32 devices in a mesh: groups: 2 (over x), row: 16 (over z, y, core).
Axes of the slice: x: 2, y: 2, z: 4, core: 2. Of those that a mesh axis runs over, the one named last changes fastest.
Arguments:
- left_proj: bfloat16 [128, 8192], P('groups', 'row'), parts along dimension 0, may hold values from -6 to 6
- right_proj: bfloat16 [128, 8192], P('groups', 'row'), parts along dimension 0, may hold values from -6 to 6
- pair_cot: bfloat16 [512, 256, 128], P(('groups', 'row')), parts along dimension 0, may hold values from -6 to 6
- out_weight: bfloat16 [1024, 128], replicated, may hold values from -0.1875 to 0.1875
Outputs:
- grad_left: bfloat16 [128, 8192], P('groups', 'row'), parts along dimension 0
- grad_right: bfloat16 [128, 8192], P('groups', 'row'), parts along dimension 0
The draws below stay inside these ranges and needn't reach their ends.
There are 2 independent parts, one for each index of `groups`. The reference program is written for one: setup_inputs(seed, part) draws one part's arguments, and reference() takes and returns one part's arrays. A program takes and returns all parts, laid end to end along the dimension named above; an argument that names none is the same for every part. Nothing has to cross between parts.
All inputs are finite; a program needn't handle non-finite values.
Results may differ from the reference program's by a relative error of at most 0.005.
Values may be sent and summed in bfloat16 or wider, within the bound.
No kernel may reach another device: no remote copies, remote signals or barrier semaphores. Data moves between devices by JAX's collectives and lax.ppermute only.
A program may use at most 128 MiB of HBM per device.

```python
import jax
import jax.numpy as jnp
from jax import lax

C = 32
P_SIZE = 128
S = 64
R = 256


def levels(own_key, extent, cuts, least, top_value):
    def one(dim, shards_of):
        steps = jax.random.uniform(jax.random.fold_in(jax.random.fold_in(own_key, 6), dim), (shards_of,), jnp.float32, least / len(cuts), top_value / len(cuts))
        return jnp.repeat(jnp.exp(steps), extent[dim] // shards_of).reshape((-1,) + (1,) * (len(extent) - dim - 1))

    gain = one(*cuts[0])
    for cut in cuts[1:]:
        gain = gain * one(*cut)
    return gain


def normal_values(key, extent, width, bound, shards=(), dtype=jnp.bfloat16):
    loudness = levels(key, extent, shards, -0.22, 0.18) if shards else 1.0
    entries = jax.random.normal(key, extent, jnp.float32) * width * loudness
    return jnp.minimum(jnp.maximum(entries, -bound), bound).astype(dtype)


def setup_inputs(seed: int = 0, part: int = 0) -> dict:
    key_of = jax.random.split(jax.random.key(seed), 5)
    own_keys = jax.random.split(jax.random.fold_in(key_of[4], part), 5)
    return {
        "left_proj": normal_values(own_keys[0], (S, R * C), 1.0, 6.0, ((1, 16),)),
        "right_proj": normal_values(own_keys[1], (S, R * C), 1.0, 6.0, ((1, 16),)),
        "pair_cot": normal_values(own_keys[2], (R, R, P_SIZE), 1.0, 6.0, ((0, 16),)),
        "out_weight": normal_values(key_of[3], (C * C, P_SIZE), (C * C) ** -0.5, 0.1875),
    }


def reference(left_proj, right_proj, pair_cot, out_weight):
    n_seq = left_proj.shape[0]
    total = pair_cot.shape[0]
    block = 16
    left = left_proj.reshape(n_seq, total, C).astype(jnp.float32)
    right = right_proj.reshape(n_seq, total, C).astype(jnp.float32)
    cot_blocks = pair_cot.reshape(total // block, block, total, P_SIZE)
    left_blocks = left.reshape(n_seq, total // block, block, C).transpose(1, 0, 2, 3)

    def step(carry, inputs):
        slab, left_blk = inputs
        prod = jnp.dot(slab.reshape(-1, P_SIZE), out_weight.T, preferred_element_type=jnp.float32)
        grad = (prod / n_seq).astype(jnp.bfloat16).astype(jnp.float32).reshape(block, total, C, C)
        row_grad = jnp.einsum('ijce,sje->sic', grad, right)
        carry = carry + jnp.einsum('ijce,sic->sje', grad, left_blk)
        return carry, row_grad

    start = jnp.zeros((n_seq, total, C), jnp.float32)
    partial_sum, row_grads = lax.scan(step, start, (cot_blocks, left_blocks))
    grad_left = row_grads.transpose(1, 0, 2, 3).reshape(n_seq, total * C).astype(jnp.bfloat16)
    grad_right = partial_sum.reshape(n_seq, total * C).astype(jnp.bfloat16)
    return grad_left, grad_right
```

```python
import math

import jax
import jax.numpy as jnp
from jax import lax
from jax.sharding import PartitionSpec as P

C = 32


def xor_pairs(n, bit):
    return [(i, i ^ (1 << bit)) for i in range(n)]


def gather_blocks(x, axis, n, bits):
    me = lax.axis_index(axis)
    buf = x[None]
    done = []
    for bit in bits:
        other = lax.ppermute(buf, axis, xor_pairs(n, bit))
        mine = (me >> bit) & 1
        low = jnp.where(mine == 0, buf, other)
        high = jnp.where(mine == 0, other, buf)
        buf = jnp.concatenate([low, high], 0)
        done = [bit] + done
    k = len(done)
    buf = buf.reshape((2,) * k + x.shape)
    order = sorted(range(k), key=lambda t: -done[t])
    buf = buf.transpose(order + list(range(k, k + x.ndim)))
    return buf.reshape((n,) + x.shape)


def scatter_sum(x, axis, n, bits):
    me = lax.axis_index(axis)
    k = n.bit_length() - 1
    buf = x.reshape((2,) * k + x.shape[1:])
    left = list(range(k - 1, -1, -1))
    for bit in bits:
        t = left.index(bit)
        mine = (me >> bit) & 1
        moved = jnp.moveaxis(buf, t, 0)
        keep = lax.dynamic_index_in_dim(moved, mine, 0, keepdims=False)
        send = lax.dynamic_index_in_dim(moved, 1 - mine, 0, keepdims=False)
        buf = keep + lax.ppermute(send, axis, xor_pairs(n, bit))
        left.pop(t)
    return buf


def index_bits(n):
    return list(range(n.bit_length() - 1))


def per_device(left_proj, right_proj, pair_cot, out_weight):
    n_seq = left_proj.shape[0]
    own_rows = pair_cot.shape[0]
    total = pair_cot.shape[1]
    p_size = pair_cot.shape[2]
    n = lax.axis_size("row")
    width = right_proj.shape[1]
    bits = index_bits(n)
    block = math.gcd(total, 256)

    right_blocks = gather_blocks(right_proj, "row", n, bits[::-1])
    right_full = right_blocks.transpose(1, 0, 2).reshape(n_seq, total, C)

    weight_ec = out_weight.reshape(C, C, p_size).transpose(1, 0, 2).reshape(C * C, p_size)

    pieces = []
    grads = []
    for begin in range(0, total, block):
        slab = pair_cot[:, begin:begin + block, :]
        prod = jnp.einsum("xk,ijk->ixj", weight_ec, slab, preferred_element_type=jnp.float32)
        grad = (prod / n_seq).astype(jnp.bfloat16)
        grad_m = grad.reshape(own_rows, C, C, block).transpose(0, 2, 1, 3).reshape(own_rows * C, C * block)
        grads.append(grad_m)
        piece = jnp.dot(left_proj, grad_m, preferred_element_type=jnp.float32)
        pieces.append(piece.reshape(n_seq, C, block).transpose(0, 2, 1))
    partial = jnp.concatenate(pieces, 1)
    partial_blocks = partial.reshape(n_seq, n, width).transpose(1, 0, 2)
    grad_right = scatter_sum(partial_blocks, "row", n, bits).astype(jnp.bfloat16)

    grad_left = jnp.zeros((n_seq, own_rows * C), jnp.float32)
    for index, begin in enumerate(range(0, total, block)):
        right_t = right_full[:, begin:begin + block, :].transpose(0, 2, 1).reshape(n_seq, C * block)
        grad_left = grad_left + lax.dot_general(
            right_t, grads[index], (((1,), (1,)), ((), ())), preferred_element_type=jnp.float32
        )
    return (grad_left.astype(jnp.bfloat16), grad_right)


def solution(mesh):
    return jax.shard_map(
        per_device,
        mesh=mesh,
        in_specs=(P("groups", "row"), P("groups", "row"), P(("groups", "row"), None, None), P()),
        out_specs=(P("groups", "row"), P("groups", "row")),
        check_vma=False,
    )
```

```python
import functools
import math

import jax
import jax.numpy as jnp
from jax import lax
from jax.experimental import pallas as pl
from jax.experimental.pallas import tpu as pltpu
from jax.sharding import PartitionSpec as P

C = 32


def xor_pairs(n, bit):
    return [(i, i ^ (1 << bit)) for i in range(n)]


def gather_blocks(x, axis, n, bits):
    me = lax.axis_index(axis)
    buf = x[None]
    done = []
    for bit in bits:
        other = lax.ppermute(buf, axis, xor_pairs(n, bit))
        mine = (me >> bit) & 1
        low = jnp.where(mine == 0, buf, other)
        high = jnp.where(mine == 0, other, buf)
        buf = jnp.concatenate([low, high], 0)
        done = [bit] + done
    k = len(done)
    buf = buf.reshape((2,) * k + x.shape)
    order = sorted(range(k), key=lambda t: -done[t])
    buf = buf.transpose(order + list(range(k, k + x.ndim)))
    return buf.reshape((n,) + x.shape)


def scatter_sum(x, axis, n, bits):
    me = lax.axis_index(axis)
    k = n.bit_length() - 1
    buf = x.reshape((2,) * k + x.shape[1:])
    left = list(range(k - 1, -1, -1))
    for bit in bits:
        t = left.index(bit)
        mine = (me >> bit) & 1
        moved = jnp.moveaxis(buf, t, 0)
        keep = lax.dynamic_index_in_dim(moved, mine, 0, keepdims=False)
        send = lax.dynamic_index_in_dim(moved, 1 - mine, 0, keepdims=False)
        buf = keep + lax.ppermute(send, axis, xor_pairs(n, bit))
        left.pop(t)
    return buf


def index_bits(n):
    return list(range(n.bit_length() - 1))


def project_kernel(p_ref, w_ref, l_ref, gm_ref, pt_ref, *, n_seq):
    rows = p_ref.shape[0]
    width = p_ref.shape[1]
    for i in range(rows):
        prod = lax.dot_general(
            w_ref[...], p_ref[i], (((1,), (1,)), ((), ())), preferred_element_type=jnp.float32
        )
        grad = (prod / n_seq).astype(jnp.bfloat16)
        for e in range(C):
            gm_ref[e, i * C:(i + 1) * C, :] = grad[e * C:(e + 1) * C, :]
    for e in range(C):
        part = lax.dot_general(
            gm_ref[e], l_ref[...], (((0,), (1,)), ((), ())), preferred_element_type=jnp.float32
        )
        pt_ref[:, e, :, :] = part.reshape(width // 16, 16, part.shape[1])


def left_kernel(gm_ref, rt_ref, out_ref):
    @pl.when(pl.program_id(0) == 0)
    def _():
        out_ref[...] = jnp.zeros_like(out_ref)

    width = gm_ref.shape[2]
    acc = out_ref[...]
    for e in range(C):
        right_e = rt_ref[:, e, :, :].reshape(width, rt_ref.shape[3]).astype(jnp.bfloat16)
        acc = acc + jnp.dot(gm_ref[e], right_e, preferred_element_type=jnp.float32)
    out_ref[...] = acc


def per_device(left_proj, right_proj, pair_cot, out_weight):
    n_seq = left_proj.shape[0]
    own_rows = pair_cot.shape[0]
    total = pair_cot.shape[1]
    p_size = pair_cot.shape[2]
    n = lax.axis_size("row")
    bits = index_bits(n)
    block = math.gcd(total, 256)
    steps = total // block
    per_dev = right_proj.shape[1] // C

    right_t = right_proj.reshape(n_seq, per_dev, C).transpose(2, 1, 0)
    right_blocks = gather_blocks(right_t, "row", n, bits[::-1]).astype(jnp.float32)

    weight_ec = out_weight.reshape(C, C, p_size).transpose(1, 0, 2).reshape(C * C, p_size)

    grad_m, part_t = pl.pallas_call(
        functools.partial(project_kernel, n_seq=n_seq),
        grid=(steps,),
        in_specs=[
            pl.BlockSpec((own_rows, block, p_size), lambda b: (0, b, 0)),
            pl.BlockSpec((C * C, p_size), lambda b: (0, 0)),
            pl.BlockSpec((n_seq, own_rows * C), lambda b: (0, 0)),
        ],
        out_specs=[
            pl.BlockSpec((C, own_rows * C, block), lambda b: (0, 0, b)),
            pl.BlockSpec((block // 16, C, 16, n_seq), lambda b: (b, 0, 0, 0)),
        ],
        out_shape=[
            jax.ShapeDtypeStruct((C, own_rows * C, total), jnp.bfloat16),
            jax.ShapeDtypeStruct((total // 16, C, 16, n_seq), jnp.float32),
        ],
        compiler_params=pltpu.CompilerParams(vmem_limit_bytes=56 * 1024 * 1024),
    )(pair_cot, weight_ec, left_proj)

    summed = scatter_sum(part_t, "row", n, bits)
    grad_right = summed.transpose(2, 1, 0).reshape(n_seq, per_dev * C).astype(jnp.bfloat16)

    left_t = pl.pallas_call(
        left_kernel,
        grid=(steps,),
        in_specs=[
            pl.BlockSpec((C, own_rows * C, block), lambda b: (0, 0, b)),
            pl.BlockSpec((block // 16, C, 16, n_seq), lambda b: (b, 0, 0, 0)),
        ],
        out_specs=pl.BlockSpec((own_rows * C, n_seq), lambda b: (0, 0)),
        out_shape=jax.ShapeDtypeStruct((own_rows * C, n_seq), jnp.float32),
        compiler_params=pltpu.CompilerParams(vmem_limit_bytes=56 * 1024 * 1024),
    )(grad_m, right_blocks)
    grad_left = left_t.T.astype(jnp.bfloat16)
    return (grad_left, grad_right)


def solution(mesh):
    return jax.shard_map(
        per_device,
        mesh=mesh,
        in_specs=(P("groups", "row"), P("groups", "row"), P(("groups", "row"), None, None), P()),
        out_specs=(P("groups", "row"), P("groups", "row")),
        check_vma=False,
    )
```

```python
import functools
import math

import jax
import jax.numpy as jnp
from jax import lax
from jax.experimental import pallas as pl
from jax.experimental.pallas import tpu as pltpu
from jax.sharding import PartitionSpec as P

C = 32


def xor_pairs(n, bit):
    return [(i, i ^ (1 << bit)) for i in range(n)]


def gather_blocks(x, axis, n, bits):
    me = lax.axis_index(axis)
    buf = x[None]
    done = []
    for bit in bits:
        other = lax.ppermute(buf, axis, xor_pairs(n, bit))
        mine = (me >> bit) & 1
        low = jnp.where(mine == 0, buf, other)
        high = jnp.where(mine == 0, other, buf)
        buf = jnp.concatenate([low, high], 0)
        done = [bit] + done
    k = len(done)
    buf = buf.reshape((2,) * k + x.shape)
    order = sorted(range(k), key=lambda t: -done[t])
    buf = buf.transpose(order + list(range(k, k + x.ndim)))
    return buf.reshape((n,) + x.shape)


def scatter_sum(x, axis, n, bits):
    me = lax.axis_index(axis)
    k = n.bit_length() - 1
    buf = x.reshape((2,) * k + x.shape[1:])
    left = list(range(k - 1, -1, -1))
    for bit in bits:
        t = left.index(bit)
        mine = (me >> bit) & 1
        moved = jnp.moveaxis(buf, t, 0)
        keep = lax.dynamic_index_in_dim(moved, mine, 0, keepdims=False)
        send = lax.dynamic_index_in_dim(moved, 1 - mine, 0, keepdims=False)
        buf = keep + lax.ppermute(send, axis, xor_pairs(n, bit))
        left.pop(t)
    return buf


def index_bits(n):
    return list(range(n.bit_length() - 1))


def project_kernel(p_ref, w_ref, l_ref, gm_ref, pt_ref, *, n_seq):
    rows = p_ref.shape[0]
    width = p_ref.shape[1]
    for i in range(rows):
        prod = lax.dot_general(
            w_ref[...], p_ref[i], (((1,), (1,)), ((), ())), preferred_element_type=jnp.float32
        )
        grad = (prod / n_seq).astype(jnp.bfloat16)
        for e in range(C):
            gm_ref[e, i * C:(i + 1) * C, :] = grad[e * C:(e + 1) * C, :]
    for e in range(C):
        part = lax.dot_general(
            gm_ref[e], l_ref[...], (((0,), (1,)), ((), ())), preferred_element_type=jnp.float32
        )
        pt_ref[:, e, :, :] = part.reshape(width // 16, 16, part.shape[1])


def left_kernel(gm_ref, rt_ref, out_ref):
    @pl.when(pl.program_id(0) == 0)
    def _():
        out_ref[...] = jnp.zeros_like(out_ref)

    width = gm_ref.shape[2]
    acc = out_ref[...]
    for e in range(C):
        right_e = rt_ref[:, e, :, :].reshape(width, rt_ref.shape[3])
        acc = acc + jnp.dot(gm_ref[e], right_e, preferred_element_type=jnp.float32)
    out_ref[...] = acc


def per_device(left_proj, right_proj, pair_cot, out_weight):
    n_seq = left_proj.shape[0]
    own_rows = pair_cot.shape[0]
    total = pair_cot.shape[1]
    p_size = pair_cot.shape[2]
    n = lax.axis_size("row")
    bits = index_bits(n)
    block = math.gcd(total, 256)
    steps = total // block
    per_dev = right_proj.shape[1] // C

    right_t = right_proj.reshape(n_seq, per_dev, C).transpose(2, 1, 0)
    right_blocks = gather_blocks(right_t, "row", n, bits[::-1])
    pair_cot, right_blocks = lax.optimization_barrier((pair_cot, right_blocks))

    weight_ec = out_weight.reshape(C, C, p_size).transpose(1, 0, 2).reshape(C * C, p_size)

    grad_m, part_t = pl.pallas_call(
        functools.partial(project_kernel, n_seq=n_seq),
        grid=(steps,),
        in_specs=[
            pl.BlockSpec((own_rows, block, p_size), lambda b: (0, b, 0)),
            pl.BlockSpec((C * C, p_size), lambda b: (0, 0)),
            pl.BlockSpec((n_seq, own_rows * C), lambda b: (0, 0)),
        ],
        out_specs=[
            pl.BlockSpec((C, own_rows * C, block), lambda b: (0, 0, b)),
            pl.BlockSpec((block // 16, C, 16, n_seq), lambda b: (b, 0, 0, 0)),
        ],
        out_shape=[
            jax.ShapeDtypeStruct((C, own_rows * C, total), jnp.bfloat16),
            jax.ShapeDtypeStruct((total // 16, C, 16, n_seq), jnp.float32),
        ],
        compiler_params=pltpu.CompilerParams(vmem_limit_bytes=56 * 1024 * 1024),
    )(pair_cot, weight_ec, left_proj)

    summed = scatter_sum(part_t, "row", n, bits)
    grad_right = summed.transpose(2, 1, 0).reshape(n_seq, per_dev * C).astype(jnp.bfloat16)

    left_t = pl.pallas_call(
        left_kernel,
        grid=(steps,),
        in_specs=[
            pl.BlockSpec((C, own_rows * C, block), lambda b: (0, 0, b)),
            pl.BlockSpec((block // 16, C, 16, n_seq), lambda b: (b, 0, 0, 0)),
        ],
        out_specs=pl.BlockSpec((own_rows * C, n_seq), lambda b: (0, 0)),
        out_shape=jax.ShapeDtypeStruct((own_rows * C, n_seq), jnp.float32),
        compiler_params=pltpu.CompilerParams(vmem_limit_bytes=56 * 1024 * 1024),
    )(grad_m, right_blocks)
    grad_left = left_t.T.astype(jnp.bfloat16)
    return (grad_left, grad_right)


def solution(mesh):
    return jax.shard_map(
        per_device,
        mesh=mesh,
        in_specs=(P("groups", "row"), P("groups", "row"), P(("groups", "row"), None, None), P()),
        out_specs=(P("groups", "row"), P("groups", "row")),
        check_vma=False,
    )
```

```python
import functools
import math

import jax
import jax.numpy as jnp
from jax import lax
from jax.experimental import pallas as pl
from jax.experimental.pallas import tpu as pltpu
from jax.sharding import PartitionSpec as P

C = 32


def xor_pairs(n, bit):
    return [(i, i ^ (1 << bit)) for i in range(n)]


def gather_blocks(x, axis, n, bits):
    me = lax.axis_index(axis)
    buf = x[None]
    done = []
    for bit in bits:
        other = lax.ppermute(buf, axis, xor_pairs(n, bit))
        mine = (me >> bit) & 1
        low = jnp.where(mine == 0, buf, other)
        high = jnp.where(mine == 0, other, buf)
        buf = jnp.concatenate([low, high], 0)
        done = [bit] + done
    k = len(done)
    buf = buf.reshape((2,) * k + x.shape)
    order = sorted(range(k), key=lambda t: -done[t])
    buf = buf.transpose(order + list(range(k, k + x.ndim)))
    return buf.reshape((n,) + x.shape)


def scatter_sum(x, axis, n, bits):
    me = lax.axis_index(axis)
    k = n.bit_length() - 1
    buf = x.reshape((2,) * k + x.shape[1:])
    left = list(range(k - 1, -1, -1))
    for bit in bits:
        t = left.index(bit)
        mine = (me >> bit) & 1
        moved = jnp.moveaxis(buf, t, 0)
        keep = lax.dynamic_index_in_dim(moved, mine, 0, keepdims=False)
        send = lax.dynamic_index_in_dim(moved, 1 - mine, 0, keepdims=False)
        buf = keep + lax.ppermute(send, axis, xor_pairs(n, bit))
        left.pop(t)
    return buf


def index_bits(n):
    return list(range(n.bit_length() - 1))


def project_kernel(p_ref, w_ref, l_ref, gm_ref, pt_ref, *, n_seq):
    rows = p_ref.shape[0]
    width = p_ref.shape[1]
    for i in range(rows):
        prod = lax.dot_general(
            w_ref[...], p_ref[i], (((1,), (1,)), ((), ())), preferred_element_type=jnp.float32
        )
        grad = (prod / n_seq).astype(jnp.bfloat16)
        for e in range(C):
            gm_ref[e, i * C:(i + 1) * C, :] = grad[e * C:(e + 1) * C, :]
    for e in range(C):
        part = lax.dot_general(
            gm_ref[e], l_ref[...], (((0,), (1,)), ((), ())), preferred_element_type=jnp.float32
        )
        pt_ref[:, e, :, :] = part.reshape(width // 16, 16, part.shape[1])


def left_kernel(gm_ref, rt_ref, out_ref):
    @pl.when(pl.program_id(0) == 0)
    def _():
        out_ref[...] = jnp.zeros_like(out_ref)

    width = gm_ref.shape[2]
    acc = out_ref[...]
    for e in range(C):
        right_e = rt_ref[:, e, :, :].reshape(width, rt_ref.shape[3])
        acc = acc + jnp.dot(gm_ref[e], right_e, preferred_element_type=jnp.float32)
    out_ref[...] = acc


def per_device(left_proj, right_proj, pair_cot, out_weight):
    n_seq = left_proj.shape[0]
    own_rows = pair_cot.shape[0]
    total = pair_cot.shape[1]
    p_size = pair_cot.shape[2]
    n = lax.axis_size("row")
    bits = index_bits(n)
    block = math.gcd(total, 256)
    steps = total // block
    per_dev = right_proj.shape[1] // C

    right_t = right_proj.reshape(n_seq, per_dev, C).transpose(2, 1, 0)
    right_blocks = lax.all_gather(right_t, "row", axis=0)

    weight_ec = out_weight.reshape(C, C, p_size).transpose(1, 0, 2).reshape(C * C, p_size)

    grad_m, part_t = pl.pallas_call(
        functools.partial(project_kernel, n_seq=n_seq),
        grid=(steps,),
        in_specs=[
            pl.BlockSpec((own_rows, block, p_size), lambda b: (0, b, 0)),
            pl.BlockSpec((C * C, p_size), lambda b: (0, 0)),
            pl.BlockSpec((n_seq, own_rows * C), lambda b: (0, 0)),
        ],
        out_specs=[
            pl.BlockSpec((C, own_rows * C, block), lambda b: (0, 0, b)),
            pl.BlockSpec((block // 16, C, 16, n_seq), lambda b: (b, 0, 0, 0)),
        ],
        out_shape=[
            jax.ShapeDtypeStruct((C, own_rows * C, total), jnp.bfloat16),
            jax.ShapeDtypeStruct((total // 16, C, 16, n_seq), jnp.float32),
        ],
        compiler_params=pltpu.CompilerParams(vmem_limit_bytes=56 * 1024 * 1024),
    )(pair_cot, weight_ec, left_proj)

    summed = scatter_sum(part_t, "row", n, bits)
    grad_right = summed.transpose(2, 1, 0).reshape(n_seq, per_dev * C).astype(jnp.bfloat16)

    left_t = pl.pallas_call(
        left_kernel,
        grid=(steps,),
        in_specs=[
            pl.BlockSpec((C, own_rows * C, block), lambda b: (0, 0, b)),
            pl.BlockSpec((block // 16, C, 16, n_seq), lambda b: (b, 0, 0, 0)),
        ],
        out_specs=pl.BlockSpec((own_rows * C, n_seq), lambda b: (0, 0)),
        out_shape=jax.ShapeDtypeStruct((own_rows * C, n_seq), jnp.float32),
        compiler_params=pltpu.CompilerParams(vmem_limit_bytes=56 * 1024 * 1024),
    )(grad_m, right_blocks)
    grad_left = left_t.T.astype(jnp.bfloat16)
    return (grad_left, grad_right)


def solution(mesh):
    return jax.shard_map(
        per_device,
        mesh=mesh,
        in_specs=(P("groups", "row"), P("groups", "row"), P(("groups", "row"), None, None), P()),
        out_specs=(P("groups", "row"), P("groups", "row")),
        check_vma=False,
    )
```

```python
import functools
import math

import jax
import jax.numpy as jnp
from jax import lax
from jax.experimental import pallas as pl
from jax.experimental.pallas import tpu as pltpu
from jax.sharding import PartitionSpec as P

C = 32


def xor_pairs(n, bit):
    return [(i, i ^ (1 << bit)) for i in range(n)]


def gather_blocks(x, axis, n, bits):
    me = lax.axis_index(axis)
    buf = x[None]
    done = []
    for bit in bits:
        other = lax.ppermute(buf, axis, xor_pairs(n, bit))
        mine = (me >> bit) & 1
        low = jnp.where(mine == 0, buf, other)
        high = jnp.where(mine == 0, other, buf)
        buf = jnp.concatenate([low, high], 0)
        done = [bit] + done
    k = len(done)
    buf = buf.reshape((2,) * k + x.shape)
    order = sorted(range(k), key=lambda t: -done[t])
    buf = buf.transpose(order + list(range(k, k + x.ndim)))
    return buf.reshape((n,) + x.shape)


def scatter_sum(x, axis, n, bits):
    me = lax.axis_index(axis)
    k = n.bit_length() - 1
    buf = x.reshape((2,) * k + x.shape[1:])
    left = list(range(k - 1, -1, -1))
    for bit in bits:
        t = left.index(bit)
        mine = (me >> bit) & 1
        moved = jnp.moveaxis(buf, t, 0)
        keep = lax.dynamic_index_in_dim(moved, mine, 0, keepdims=False)
        send = lax.dynamic_index_in_dim(moved, 1 - mine, 0, keepdims=False)
        buf = keep + lax.ppermute(send, axis, xor_pairs(n, bit))
        left.pop(t)
    return buf


def index_bits(n):
    return list(range(n.bit_length() - 1))


def project_kernel(p_ref, w_ref, l_ref, gm_ref, pt_ref, *, n_seq):
    rows = p_ref.shape[0]
    width = p_ref.shape[1]
    for i in range(rows):
        prod = lax.dot_general(
            w_ref[...], p_ref[i], (((1,), (1,)), ((), ())), preferred_element_type=jnp.float32
        )
        grad = (prod / n_seq).astype(jnp.bfloat16)
        for e in range(C):
            gm_ref[e, i * C:(i + 1) * C, :] = grad[e * C:(e + 1) * C, :]
    for e in range(C):
        part = lax.dot_general(
            gm_ref[e], l_ref[...], (((0,), (1,)), ((), ())), preferred_element_type=jnp.float32
        )
        pt_ref[:, e, :, :] = part.reshape(width // 16, 16, part.shape[1])


def left_kernel(gm_ref, rt_ref, out_ref):
    @pl.when(pl.program_id(0) == 0)
    def _():
        out_ref[...] = jnp.zeros_like(out_ref)

    width = gm_ref.shape[2]
    acc = out_ref[...]
    for e in range(C):
        right_e = rt_ref[:, e, :, :].reshape(width, rt_ref.shape[3])
        acc = acc + jnp.dot(gm_ref[e], right_e, preferred_element_type=jnp.float32)
    out_ref[...] = acc


def per_device(left_proj, right_proj, pair_cot, out_weight):
    n_seq = left_proj.shape[0]
    own_rows = pair_cot.shape[0]
    total = pair_cot.shape[1]
    p_size = pair_cot.shape[2]
    n = lax.axis_size("row")
    bits = index_bits(n)
    block = math.gcd(total, 256)
    steps = total // block
    per_dev = right_proj.shape[1] // C

    right_t = right_proj.reshape(n_seq, per_dev, C).transpose(2, 1, 0)
    right_blocks = gather_blocks(right_t, "row", n, bits[::-1])

    weight_ec = out_weight.reshape(C, C, p_size).transpose(1, 0, 2).reshape(C * C, p_size)

    grad_m, part_t = pl.pallas_call(
        functools.partial(project_kernel, n_seq=n_seq),
        grid=(steps,),
        in_specs=[
            pl.BlockSpec((own_rows, block, p_size), lambda b: (0, b, 0)),
            pl.BlockSpec((C * C, p_size), lambda b: (0, 0)),
            pl.BlockSpec((n_seq, own_rows * C), lambda b: (0, 0)),
        ],
        out_specs=[
            pl.BlockSpec((C, own_rows * C, block), lambda b: (0, 0, b)),
            pl.BlockSpec((block // 16, C, 16, n_seq), lambda b: (b, 0, 0, 0)),
        ],
        out_shape=[
            jax.ShapeDtypeStruct((C, own_rows * C, total), jnp.bfloat16),
            jax.ShapeDtypeStruct((total // 16, C, 16, n_seq), jnp.float32),
        ],
        compiler_params=pltpu.CompilerParams(vmem_limit_bytes=56 * 1024 * 1024),
        cost_estimate=pl.CostEstimate(
            flops=2 * own_rows * total * C * C * (p_size + n_seq),
            transcendentals=0,
            bytes_accessed=2 * own_rows * total * (p_size + C * C) + 4 * total * C * n_seq,
        ),
    )(pair_cot, weight_ec, left_proj)

    summed = scatter_sum(part_t, "row", n, bits)
    grad_right = summed.transpose(2, 1, 0).reshape(n_seq, per_dev * C).astype(jnp.bfloat16)

    left_t = pl.pallas_call(
        left_kernel,
        grid=(steps,),
        in_specs=[
            pl.BlockSpec((C, own_rows * C, block), lambda b: (0, 0, b)),
            pl.BlockSpec((block // 16, C, 16, n_seq), lambda b: (b, 0, 0, 0)),
        ],
        out_specs=pl.BlockSpec((own_rows * C, n_seq), lambda b: (0, 0)),
        out_shape=jax.ShapeDtypeStruct((own_rows * C, n_seq), jnp.float32),
        compiler_params=pltpu.CompilerParams(vmem_limit_bytes=56 * 1024 * 1024),
        cost_estimate=pl.CostEstimate(
            flops=2 * own_rows * total * C * C * n_seq,
            transcendentals=0,
            bytes_accessed=2 * own_rows * total * C * C + 2 * total * C * n_seq,
        ),
    )(grad_m, right_blocks)
    grad_left = left_t.T.astype(jnp.bfloat16)
    return (grad_left, grad_right)


def solution(mesh):
    return jax.shard_map(
        per_device,
        mesh=mesh,
        in_specs=(P("groups", "row"), P("groups", "row"), P(("groups", "row"), None, None), P()),
        out_specs=(P("groups", "row"), P("groups", "row")),
        check_vma=False,
    )
```

```python
import functools
import math

import jax
import jax.numpy as jnp
from jax import lax
from jax.experimental import pallas as pl
from jax.experimental.pallas import tpu as pltpu
from jax.sharding import PartitionSpec as P

C = 32


def xor_pairs(n, bit):
    return [(i, i ^ (1 << bit)) for i in range(n)]


def gather_blocks(x, axis, n, bits):
    me = lax.axis_index(axis)
    buf = x[None]
    done = []
    for bit in bits:
        other = lax.ppermute(buf, axis, xor_pairs(n, bit))
        mine = (me >> bit) & 1
        low = jnp.where(mine == 0, buf, other)
        high = jnp.where(mine == 0, other, buf)
        buf = jnp.concatenate([low, high], 0)
        done = [bit] + done
    k = len(done)
    buf = buf.reshape((2,) * k + x.shape)
    order = sorted(range(k), key=lambda t: -done[t])
    buf = buf.transpose(order + list(range(k, k + x.ndim)))
    return buf.reshape((n,) + x.shape)


def scatter_sum(x, axis, n, bits):
    me = lax.axis_index(axis)
    k = n.bit_length() - 1
    buf = x.reshape((2,) * k + x.shape[1:])
    left = list(range(k - 1, -1, -1))
    for bit in bits:
        t = left.index(bit)
        mine = (me >> bit) & 1
        moved = jnp.moveaxis(buf, t, 0)
        keep = lax.dynamic_index_in_dim(moved, mine, 0, keepdims=False)
        send = lax.dynamic_index_in_dim(moved, 1 - mine, 0, keepdims=False)
        buf = keep + lax.ppermute(send, axis, xor_pairs(n, bit))
        left.pop(t)
    return buf


def index_bits(n):
    return list(range(n.bit_length() - 1))


def project_kernel(p_ref, w_ref, l_ref, gm_ref, pt_ref, *, n_seq):
    rows = p_ref.shape[0]
    width = p_ref.shape[1]
    for i in range(rows):
        prod = lax.dot_general(
            w_ref[...], p_ref[i], (((1,), (1,)), ((), ())), preferred_element_type=jnp.float32
        )
        grad = (prod / n_seq).astype(jnp.bfloat16)
        for e in range(C):
            gm_ref[e, i * C:(i + 1) * C, :] = grad[e * C:(e + 1) * C, :]
    for e in range(C):
        part = lax.dot_general(
            gm_ref[e], l_ref[...], (((0,), (1,)), ((), ())), preferred_element_type=jnp.float32
        )
        pt_ref[:, e, :, :] = part.reshape(width // 16, 16, part.shape[1])


def left_kernel(gm_ref, rt_ref, out_ref):
    @pl.when(pl.program_id(0) == 0)
    def _():
        out_ref[...] = jnp.zeros_like(out_ref)

    width = gm_ref.shape[2]
    acc = out_ref[...]
    for e in range(C):
        right_e = rt_ref[:, e, :, :].reshape(width, rt_ref.shape[3])
        acc = acc + jnp.dot(gm_ref[e], right_e, preferred_element_type=jnp.float32)
    out_ref[...] = acc


def per_device(left_proj, right_proj, pair_cot, out_weight):
    n_seq = left_proj.shape[0]
    own_rows = pair_cot.shape[0]
    total = pair_cot.shape[1]
    p_size = pair_cot.shape[2]
    n = lax.axis_size("row")
    bits = index_bits(n)
    block = math.gcd(total, 256)
    steps = total // block
    per_dev = right_proj.shape[1] // C

    right_t = right_proj.reshape(n_seq, per_dev, C).transpose(2, 1, 0)
    right_blocks = jnp.concatenate(
        [
            gather_blocks(right_t[:C // 2], "row", n, bits[::-1]),
            gather_blocks(right_t[C // 2:], "row", n, (bits[:1] + bits[1:3][::-1] + bits[3:])[::-1]),
        ],
        1,
    )

    weight_ec = out_weight.reshape(C, C, p_size).transpose(1, 0, 2).reshape(C * C, p_size)

    grad_m, part_t = pl.pallas_call(
        functools.partial(project_kernel, n_seq=n_seq),
        grid=(steps,),
        in_specs=[
            pl.BlockSpec((own_rows, block, p_size), lambda b: (0, b, 0)),
            pl.BlockSpec((C * C, p_size), lambda b: (0, 0)),
            pl.BlockSpec((n_seq, own_rows * C), lambda b: (0, 0)),
        ],
        out_specs=[
            pl.BlockSpec((C, own_rows * C, block), lambda b: (0, 0, b)),
            pl.BlockSpec((block // 16, C, 16, n_seq), lambda b: (b, 0, 0, 0)),
        ],
        out_shape=[
            jax.ShapeDtypeStruct((C, own_rows * C, total), jnp.bfloat16),
            jax.ShapeDtypeStruct((total // 16, C, 16, n_seq), jnp.float32),
        ],
        compiler_params=pltpu.CompilerParams(vmem_limit_bytes=56 * 1024 * 1024),
        cost_estimate=pl.CostEstimate(
            flops=2 * own_rows * total * C * C * (p_size + n_seq),
            transcendentals=0,
            bytes_accessed=2 * own_rows * total * (p_size + C * C) + 4 * total * C * n_seq,
        ),
    )(pair_cot, weight_ec, left_proj)

    half = C // 2
    swapped = bits[:1] + bits[1:3][::-1] + bits[3:]
    summed = jnp.concatenate(
        [
            scatter_sum(part_t[:, :half], "row", n, bits),
            scatter_sum(part_t[:, half:], "row", n, swapped),
        ],
        0,
    )
    grad_right = summed.transpose(2, 1, 0).reshape(n_seq, per_dev * C).astype(jnp.bfloat16)

    left_t = pl.pallas_call(
        left_kernel,
        grid=(steps,),
        in_specs=[
            pl.BlockSpec((C, own_rows * C, block), lambda b: (0, 0, b)),
            pl.BlockSpec((block // 16, C, 16, n_seq), lambda b: (b, 0, 0, 0)),
        ],
        out_specs=pl.BlockSpec((own_rows * C, n_seq), lambda b: (0, 0)),
        out_shape=jax.ShapeDtypeStruct((own_rows * C, n_seq), jnp.float32),
        compiler_params=pltpu.CompilerParams(vmem_limit_bytes=56 * 1024 * 1024),
        cost_estimate=pl.CostEstimate(
            flops=2 * own_rows * total * C * C * n_seq,
            transcendentals=0,
            bytes_accessed=2 * own_rows * total * C * C + 2 * total * C * n_seq,
        ),
    )(grad_m, right_blocks)
    grad_left = left_t.T.astype(jnp.bfloat16)
    return (grad_left, grad_right)


def solution(mesh):
    return jax.shard_map(
        per_device,
        mesh=mesh,
        in_specs=(P("groups", "row"), P("groups", "row"), P(("groups", "row"), None, None), P()),
        out_specs=(P("groups", "row"), P("groups", "row")),
        check_vma=False,
    )
```

```python
import functools
import math

import jax
import jax.numpy as jnp
from jax import lax
from jax.experimental import pallas as pl
from jax.experimental.pallas import tpu as pltpu
from jax.sharding import PartitionSpec as P

C = 32


def xor_pairs(n, bit):
    return [(i, i ^ (1 << bit)) for i in range(n)]


def gather_blocks(x, axis, n, bits):
    me = lax.axis_index(axis)
    buf = x[None]
    done = []
    for bit in bits:
        other = lax.ppermute(buf, axis, xor_pairs(n, bit))
        mine = (me >> bit) & 1
        low = jnp.where(mine == 0, buf, other)
        high = jnp.where(mine == 0, other, buf)
        buf = jnp.concatenate([low, high], 0)
        done = [bit] + done
    k = len(done)
    buf = buf.reshape((2,) * k + x.shape)
    order = sorted(range(k), key=lambda t: -done[t])
    buf = buf.transpose(order + list(range(k, k + x.ndim)))
    return buf.reshape((n,) + x.shape)


def scatter_sum(x, axis, n, bits):
    me = lax.axis_index(axis)
    k = n.bit_length() - 1
    buf = x.reshape((2,) * k + x.shape[1:])
    left = list(range(k - 1, -1, -1))
    for bit in bits:
        t = left.index(bit)
        mine = (me >> bit) & 1
        moved = jnp.moveaxis(buf, t, 0)
        keep = lax.dynamic_index_in_dim(moved, mine, 0, keepdims=False)
        send = lax.dynamic_index_in_dim(moved, 1 - mine, 0, keepdims=False)
        buf = keep + lax.ppermute(send, axis, xor_pairs(n, bit))
        left.pop(t)
    return buf


def index_bits(n):
    return list(range(n.bit_length() - 1))


def project_kernel(p_ref, w_ref, l_ref, gm_ref, pt_ref, *, n_seq):
    rows = p_ref.shape[0]
    width = p_ref.shape[1]
    for i in range(rows):
        prod = lax.dot_general(
            w_ref[...], p_ref[i], (((1,), (1,)), ((), ())), preferred_element_type=jnp.float32
        )
        grad = (prod / n_seq).astype(jnp.bfloat16)
        for e in range(C):
            gm_ref[e, i * C:(i + 1) * C, :] = grad[e * C:(e + 1) * C, :]
    for e in range(C):
        part = lax.dot_general(
            gm_ref[e], l_ref[...], (((0,), (1,)), ((), ())), preferred_element_type=jnp.float32
        )
        pt_ref[:, e, :, :] = part.reshape(width // 16, 16, part.shape[1])


def left_kernel(gm_ref, rt_ref, out_ref):
    @pl.when(pl.program_id(0) == 0)
    def _():
        out_ref[...] = jnp.zeros_like(out_ref)

    width = gm_ref.shape[2]
    acc = out_ref[...]
    for e in range(C):
        right_e = rt_ref[:, e, :, :].reshape(width, rt_ref.shape[3])
        acc = acc + jnp.dot(gm_ref[e], right_e, preferred_element_type=jnp.float32)
    out_ref[...] = acc


def per_device(left_proj, right_proj, pair_cot, out_weight):
    n_seq = left_proj.shape[0]
    own_rows = pair_cot.shape[0]
    total = pair_cot.shape[1]
    p_size = pair_cot.shape[2]
    n = lax.axis_size("row")
    bits = index_bits(n)
    block = math.gcd(total, 256)
    steps = total // block
    per_dev = right_proj.shape[1] // C

    right_t = right_proj.reshape(n_seq, per_dev, C).transpose(2, 1, 0)
    right_blocks = jnp.concatenate(
        [
            gather_blocks(right_t[:C // 2], "row", n, bits[::-1]),
            gather_blocks(right_t[C // 2:], "row", n, (bits[:1] + bits[1:3][::-1] + bits[3:])[::-1]),
        ],
        1,
    )

    weight_ec = out_weight.reshape(C, C, p_size).transpose(1, 0, 2).reshape(C * C, p_size)

    grad_m, part_t = pl.pallas_call(
        functools.partial(project_kernel, n_seq=n_seq),
        grid=(steps,),
        in_specs=[
            pl.BlockSpec((own_rows, block, p_size), lambda b: (0, b, 0)),
            pl.BlockSpec((C * C, p_size), lambda b: (0, 0)),
            pl.BlockSpec((n_seq, own_rows * C), lambda b: (0, 0)),
        ],
        out_specs=[
            pl.BlockSpec((C, own_rows * C, block), lambda b: (0, 0, b)),
            pl.BlockSpec((block // 16, C, 16, n_seq), lambda b: (b, 0, 0, 0)),
        ],
        out_shape=[
            jax.ShapeDtypeStruct((C, own_rows * C, total), jnp.bfloat16),
            jax.ShapeDtypeStruct((total // 16, C, 16, n_seq), jnp.float32),
        ],
        compiler_params=pltpu.CompilerParams(vmem_limit_bytes=56 * 1024 * 1024),
        cost_estimate=pl.CostEstimate(
            flops=2 * own_rows * total * C * C * (p_size + n_seq),
            transcendentals=0,
            bytes_accessed=2 * own_rows * total * (p_size + C * C) + 4 * total * C * n_seq,
        ),
    )(pair_cot, weight_ec, left_proj)

    pieces = 4
    size = C // pieces
    swapped = bits[:1] + bits[1:3][::-1] + bits[3:]
    summed = jnp.concatenate(
        [
            scatter_sum(part_t[:, q * size:(q + 1) * size], "row", n, swapped if q % 2 else bits)
            for q in range(pieces)
        ],
        0,
    )
    grad_right = summed.transpose(2, 1, 0).reshape(n_seq, per_dev * C).astype(jnp.bfloat16)

    left_t = pl.pallas_call(
        left_kernel,
        grid=(steps,),
        in_specs=[
            pl.BlockSpec((C, own_rows * C, block), lambda b: (0, 0, b)),
            pl.BlockSpec((block // 16, C, 16, n_seq), lambda b: (b, 0, 0, 0)),
        ],
        out_specs=pl.BlockSpec((own_rows * C, n_seq), lambda b: (0, 0)),
        out_shape=jax.ShapeDtypeStruct((own_rows * C, n_seq), jnp.float32),
        compiler_params=pltpu.CompilerParams(vmem_limit_bytes=56 * 1024 * 1024),
        cost_estimate=pl.CostEstimate(
            flops=2 * own_rows * total * C * C * n_seq,
            transcendentals=0,
            bytes_accessed=2 * own_rows * total * C * C + 2 * total * C * n_seq,
        ),
    )(grad_m, right_blocks)
    grad_left = left_t.T.astype(jnp.bfloat16)
    return (grad_left, grad_right)


def solution(mesh):
    return jax.shard_map(
        per_device,
        mesh=mesh,
        in_specs=(P("groups", "row"), P("groups", "row"), P(("groups", "row"), None, None), P()),
        out_specs=(P("groups", "row"), P("groups", "row")),
        check_vma=False,
    )
```

```python
import functools
import math

import jax
import jax.numpy as jnp
from jax import lax
from jax.experimental import pallas as pl
from jax.experimental.pallas import tpu as pltpu
from jax.sharding import PartitionSpec as P

C = 32


def xor_pairs(n, bit):
    return [(i, i ^ (1 << bit)) for i in range(n)]


def gather_blocks(x, axis, n, bits):
    me = lax.axis_index(axis)
    buf = x[None]
    done = []
    for bit in bits:
        other = lax.ppermute(buf, axis, xor_pairs(n, bit))
        mine = (me >> bit) & 1
        low = jnp.where(mine == 0, buf, other)
        high = jnp.where(mine == 0, other, buf)
        buf = jnp.concatenate([low, high], 0)
        done = [bit] + done
    k = len(done)
    buf = buf.reshape((2,) * k + x.shape)
    order = sorted(range(k), key=lambda t: -done[t])
    buf = buf.transpose(order + list(range(k, k + x.ndim)))
    return buf.reshape((n,) + x.shape)


def scatter_sum(x, axis, n, bits):
    me = lax.axis_index(axis)
    k = n.bit_length() - 1
    buf = x.reshape((2,) * k + x.shape[1:])
    left = list(range(k - 1, -1, -1))
    for bit in bits:
        t = left.index(bit)
        mine = (me >> bit) & 1
        moved = jnp.moveaxis(buf, t, 0)
        keep = lax.dynamic_index_in_dim(moved, mine, 0, keepdims=False)
        send = lax.dynamic_index_in_dim(moved, 1 - mine, 0, keepdims=False)
        buf = keep + lax.ppermute(send, axis, xor_pairs(n, bit))
        left.pop(t)
    return buf


def index_bits(n):
    return list(range(n.bit_length() - 1))


def project_kernel(p_ref, w_ref, l_ref, gm_ref, pt_ref, *, n_seq):
    rows = p_ref.shape[0]
    width = p_ref.shape[1]
    for i in range(rows):
        prod = lax.dot_general(
            w_ref[...], p_ref[i], (((1,), (1,)), ((), ())), preferred_element_type=jnp.float32
        )
        grad = (prod / n_seq).astype(jnp.bfloat16)
        for e in range(C):
            gm_ref[e, i * C:(i + 1) * C, :] = grad[e * C:(e + 1) * C, :]
    for e in range(C):
        part = lax.dot_general(
            gm_ref[e], l_ref[...], (((0,), (1,)), ((), ())), preferred_element_type=jnp.float32
        )
        pt_ref[:, e, :, :] = part.reshape(width // 16, 16, part.shape[1])


def left_kernel(gm_ref, rt_ref, out_ref):
    @pl.when(pl.program_id(0) == 0)
    def _():
        out_ref[...] = jnp.zeros_like(out_ref)

    width = gm_ref.shape[2]
    acc = out_ref[...]
    for e in range(C):
        right_e = rt_ref[:, e, :, :].reshape(width, rt_ref.shape[3])
        acc = acc + jnp.dot(gm_ref[e], right_e, preferred_element_type=jnp.float32)
    out_ref[...] = acc


def per_device(left_proj, right_proj, pair_cot, out_weight):
    n_seq = left_proj.shape[0]
    own_rows = pair_cot.shape[0]
    total = pair_cot.shape[1]
    p_size = pair_cot.shape[2]
    n = lax.axis_size("row")
    bits = index_bits(n)
    block = math.gcd(total, 256)
    steps = total // block
    per_dev = right_proj.shape[1] // C

    right_t = right_proj.reshape(n_seq, per_dev, C).transpose(2, 1, 0)
    right_blocks = jnp.concatenate(
        [
            gather_blocks(right_t[:C // 2], "row", n, bits[::-1]),
            gather_blocks(right_t[C // 2:], "row", n, (bits[:1] + bits[1:3][::-1] + bits[3:])[::-1]),
        ],
        1,
    )

    weight_ec = out_weight.reshape(C, C, p_size).transpose(1, 0, 2).reshape(C * C, p_size)

    grad_m, part_t = pl.pallas_call(
        functools.partial(project_kernel, n_seq=n_seq),
        grid=(steps,),
        in_specs=[
            pl.BlockSpec((own_rows, block, p_size), lambda b: (0, b, 0)),
            pl.BlockSpec((C * C, p_size), lambda b: (0, 0)),
            pl.BlockSpec((n_seq, own_rows * C), lambda b: (0, 0)),
        ],
        out_specs=[
            pl.BlockSpec((C, own_rows * C, block), lambda b: (0, 0, b)),
            pl.BlockSpec((block // 16, C, 16, n_seq), lambda b: (b, 0, 0, 0)),
        ],
        out_shape=[
            jax.ShapeDtypeStruct((C, own_rows * C, total), jnp.bfloat16),
            jax.ShapeDtypeStruct((total // 16, C, 16, n_seq), jnp.float32),
        ],
        compiler_params=pltpu.CompilerParams(vmem_limit_bytes=56 * 1024 * 1024),
        cost_estimate=pl.CostEstimate(
            flops=2 * own_rows * total * C * C * (p_size + n_seq),
            transcendentals=0,
            bytes_accessed=2 * own_rows * total * (p_size + C * C) + 4 * total * C * n_seq,
        ),
    )(pair_cot, weight_ec, left_proj)

    half = C // 2
    swapped = bits[:1] + bits[1:3][::-1] + bits[3:]
    summed = jnp.concatenate(
        [
            scatter_sum(part_t[:, :half], "row", n, bits),
            scatter_sum(part_t[:, half:], "row", n, swapped),
        ],
        0,
    )
    grad_right = summed.transpose(2, 1, 0).reshape(n_seq, per_dev * C).astype(jnp.bfloat16)
    grad_m, grad_right = lax.optimization_barrier((grad_m, grad_right))

    left_t = pl.pallas_call(
        left_kernel,
        grid=(steps,),
        in_specs=[
            pl.BlockSpec((C, own_rows * C, block), lambda b: (0, 0, b)),
            pl.BlockSpec((block // 16, C, 16, n_seq), lambda b: (b, 0, 0, 0)),
        ],
        out_specs=pl.BlockSpec((own_rows * C, n_seq), lambda b: (0, 0)),
        out_shape=jax.ShapeDtypeStruct((own_rows * C, n_seq), jnp.float32),
        compiler_params=pltpu.CompilerParams(vmem_limit_bytes=56 * 1024 * 1024),
        cost_estimate=pl.CostEstimate(
            flops=2 * own_rows * total * C * C * n_seq,
            transcendentals=0,
            bytes_accessed=2 * own_rows * total * C * C + 2 * total * C * n_seq,
        ),
    )(grad_m, right_blocks)
    grad_left = left_t.T.astype(jnp.bfloat16)
    return (grad_left, grad_right)


def solution(mesh):
    return jax.shard_map(
        per_device,
        mesh=mesh,
        in_specs=(P("groups", "row"), P("groups", "row"), P(("groups", "row"), None, None), P()),
        out_specs=(P("groups", "row"), P("groups", "row")),
        check_vma=False,
    )
```

```python
import functools
import math

import jax
import jax.numpy as jnp
from jax import lax
from jax.experimental import pallas as pl
from jax.experimental.pallas import tpu as pltpu
from jax.sharding import PartitionSpec as P

C = 32


def xor_pairs(n, bit):
    return [(i, i ^ (1 << bit)) for i in range(n)]


def gather_blocks(x, axis, n, bits):
    me = lax.axis_index(axis)
    buf = x[None]
    done = []
    for bit in bits:
        other = lax.ppermute(buf, axis, xor_pairs(n, bit))
        mine = (me >> bit) & 1
        low = jnp.where(mine == 0, buf, other)
        high = jnp.where(mine == 0, other, buf)
        buf = jnp.concatenate([low, high], 0)
        done = [bit] + done
    k = len(done)
    buf = buf.reshape((2,) * k + x.shape)
    order = sorted(range(k), key=lambda t: -done[t])
    buf = buf.transpose(order + list(range(k, k + x.ndim)))
    return buf.reshape((n,) + x.shape)


def scatter_sum(x, axis, n, bits):
    me = lax.axis_index(axis)
    k = n.bit_length() - 1
    buf = x.reshape((2,) * k + x.shape[1:])
    left = list(range(k - 1, -1, -1))
    for bit in bits:
        t = left.index(bit)
        mine = (me >> bit) & 1
        moved = jnp.moveaxis(buf, t, 0)
        keep = lax.dynamic_index_in_dim(moved, mine, 0, keepdims=False)
        send = lax.dynamic_index_in_dim(moved, 1 - mine, 0, keepdims=False)
        buf = keep + lax.ppermute(send, axis, xor_pairs(n, bit))
        left.pop(t)
    return buf


def scatter_sum_ordered(x, axis, bits):
    me = lax.axis_index(axis)
    n = x.shape[0]
    buf = x
    for bit in bits:
        half = buf.shape[0] // 2
        mine = (me >> bit) & 1
        keep = lax.dynamic_slice_in_dim(buf, mine * half, half, 0)
        send = lax.dynamic_slice_in_dim(buf, (1 - mine) * half, half, 0)
        buf = keep + lax.ppermute(send, axis, xor_pairs(n, bit))
    return buf[0]


def position(d, bits):
    k = len(bits)
    return sum(((d >> bit) & 1) << (k - 1 - t) for t, bit in enumerate(bits))


def index_bits(n):
    return list(range(n.bit_length() - 1))


def project_kernel(p_ref, w_ref, l_ref, gm_ref, pt_ref, *, n_seq, orders):
    rows = p_ref.shape[0]
    width = p_ref.shape[1]
    per_block = width // 16
    half = C // len(orders)
    for i in range(rows):
        prod = lax.dot_general(
            w_ref[...], p_ref[i], (((1,), (1,)), ((), ())), preferred_element_type=jnp.float32
        )
        grad = (prod / n_seq).astype(jnp.bfloat16)
        for e in range(C):
            gm_ref[e, i * C:(i + 1) * C, :] = grad[e * C:(e + 1) * C, :]
    first = pl.program_id(0) * per_block
    for e in range(C):
        part = lax.dot_general(
            gm_ref[e], l_ref[...], (((0,), (1,)), ((), ())), preferred_element_type=jnp.float32
        )
        part = part.reshape(per_block, 16, part.shape[1])
        h = e // half
        for local in range(per_block):
            pt_ref[h, position(first + local, orders[h]), e % half] = part[local]


def left_kernel(gm_ref, rt_ref, out_ref):
    @pl.when(pl.program_id(0) == 0)
    def _():
        out_ref[...] = jnp.zeros_like(out_ref)

    width = gm_ref.shape[2]
    acc = out_ref[...]
    for e in range(C):
        right_e = rt_ref[:, e, :, :].reshape(width, rt_ref.shape[3])
        acc = acc + jnp.dot(gm_ref[e], right_e, preferred_element_type=jnp.float32)
    out_ref[...] = acc


def per_device(left_proj, right_proj, pair_cot, out_weight):
    n_seq = left_proj.shape[0]
    own_rows = pair_cot.shape[0]
    total = pair_cot.shape[1]
    p_size = pair_cot.shape[2]
    n = lax.axis_size("row")
    bits = index_bits(n)
    block = math.gcd(total, 256)
    steps = total // block
    per_dev = right_proj.shape[1] // C

    right_t = right_proj.reshape(n_seq, per_dev, C).transpose(2, 1, 0)
    right_blocks = jnp.concatenate(
        [
            gather_blocks(right_t[:C // 2], "row", n, bits[::-1]),
            gather_blocks(right_t[C // 2:], "row", n, (bits[:1] + bits[1:3][::-1] + bits[3:])[::-1]),
        ],
        1,
    )

    weight_ec = out_weight.reshape(C, C, p_size).transpose(1, 0, 2).reshape(C * C, p_size)

    swapped = bits[:1] + bits[1:3][::-1] + bits[3:]
    orders = (tuple(bits), tuple(swapped))
    half = C // len(orders)
    grad_m, part_t = pl.pallas_call(
        functools.partial(project_kernel, n_seq=n_seq, orders=orders),
        grid=(steps,),
        in_specs=[
            pl.BlockSpec((own_rows, block, p_size), lambda b: (0, b, 0)),
            pl.BlockSpec((C * C, p_size), lambda b: (0, 0)),
            pl.BlockSpec((n_seq, own_rows * C), lambda b: (0, 0)),
        ],
        out_specs=[
            pl.BlockSpec((C, own_rows * C, block), lambda b: (0, 0, b)),
            pl.BlockSpec((len(orders), total // 16, half, 16, n_seq), lambda b: (0, 0, 0, 0, 0)),
        ],
        out_shape=[
            jax.ShapeDtypeStruct((C, own_rows * C, total), jnp.bfloat16),
            jax.ShapeDtypeStruct((len(orders), total // 16, half, 16, n_seq), jnp.float32),
        ],
        compiler_params=pltpu.CompilerParams(vmem_limit_bytes=56 * 1024 * 1024),
        cost_estimate=pl.CostEstimate(
            flops=2 * own_rows * total * C * C * (p_size + n_seq),
            transcendentals=0,
            bytes_accessed=2 * own_rows * total * (p_size + C * C) + 4 * total * C * n_seq,
        ),
    )(pair_cot, weight_ec, left_proj)

    summed = jnp.concatenate(
        [scatter_sum_ordered(part_t[h], "row", list(orders[h])) for h in range(len(orders))], 0
    )
    grad_right = summed.transpose(2, 1, 0).reshape(n_seq, per_dev * C).astype(jnp.bfloat16)

    left_t = pl.pallas_call(
        left_kernel,
        grid=(steps,),
        in_specs=[
            pl.BlockSpec((C, own_rows * C, block), lambda b: (0, 0, b)),
            pl.BlockSpec((block // 16, C, 16, n_seq), lambda b: (b, 0, 0, 0)),
        ],
        out_specs=pl.BlockSpec((own_rows * C, n_seq), lambda b: (0, 0)),
        out_shape=jax.ShapeDtypeStruct((own_rows * C, n_seq), jnp.float32),
        compiler_params=pltpu.CompilerParams(vmem_limit_bytes=56 * 1024 * 1024),
        cost_estimate=pl.CostEstimate(
            flops=2 * own_rows * total * C * C * n_seq,
            transcendentals=0,
            bytes_accessed=2 * own_rows * total * C * C + 2 * total * C * n_seq,
        ),
    )(grad_m, right_blocks)
    grad_left = left_t.T.astype(jnp.bfloat16)
    return (grad_left, grad_right)


def solution(mesh):
    return jax.shard_map(
        per_device,
        mesh=mesh,
        in_specs=(P("groups", "row"), P("groups", "row"), P(("groups", "row"), None, None), P()),
        out_specs=(P("groups", "row"), P("groups", "row")),
        check_vma=False,
    )
```

```python
import functools
import math

import jax
import jax.numpy as jnp
from jax import lax
from jax.experimental import pallas as pl
from jax.experimental.pallas import tpu as pltpu
from jax.sharding import PartitionSpec as P

C = 32


def xor_pairs(n, bit):
    return [(i, i ^ (1 << bit)) for i in range(n)]


def gather_blocks(x, axis, n, bits):
    me = lax.axis_index(axis)
    buf = x[None]
    done = []
    for bit in bits:
        other = lax.ppermute(buf, axis, xor_pairs(n, bit))
        mine = (me >> bit) & 1
        low = jnp.where(mine == 0, buf, other)
        high = jnp.where(mine == 0, other, buf)
        buf = jnp.concatenate([low, high], 0)
        done = [bit] + done
    k = len(done)
    buf = buf.reshape((2,) * k + x.shape)
    order = sorted(range(k), key=lambda t: -done[t])
    buf = buf.transpose(order + list(range(k, k + x.ndim)))
    return buf.reshape((n,) + x.shape)


def scatter_sum(x, axis, n, bits):
    me = lax.axis_index(axis)
    k = n.bit_length() - 1
    buf = x.reshape((2,) * k + x.shape[1:])
    left = list(range(k - 1, -1, -1))
    for bit in bits:
        t = left.index(bit)
        mine = (me >> bit) & 1
        moved = jnp.moveaxis(buf, t, 0)
        keep = lax.dynamic_index_in_dim(moved, mine, 0, keepdims=False)
        send = lax.dynamic_index_in_dim(moved, 1 - mine, 0, keepdims=False)
        buf = keep + lax.ppermute(send, axis, xor_pairs(n, bit))
        left.pop(t)
    return buf


def gather_step(state, axis, n, bit):
    buf, done = state
    me = lax.axis_index(axis)
    other = lax.ppermute(buf, axis, xor_pairs(n, bit))
    mine = (me >> bit) & 1
    low = jnp.where(mine == 0, buf, other)
    high = jnp.where(mine == 0, other, buf)
    return jnp.concatenate([low, high], 0), [bit] + done


def gather_finish(state, n, shape):
    buf, done = state
    k = len(done)
    buf = buf.reshape((2,) * k + shape)
    order = sorted(range(k), key=lambda t: -done[t])
    buf = buf.transpose(order + list(range(k, k + len(shape))))
    return buf.reshape((n,) + shape)


def scatter_step(buf, axis, n, bit):
    me = lax.axis_index(axis)
    half = buf.shape[0] // 2
    mine = (me >> bit) & 1
    keep = lax.dynamic_slice_in_dim(buf, mine * half, half, 0)
    send = lax.dynamic_slice_in_dim(buf, (1 - mine) * half, half, 0)
    return keep + lax.ppermute(send, axis, xor_pairs(n, bit))


def scatter_sum_ordered(x, axis, bits):
    me = lax.axis_index(axis)
    n = x.shape[0]
    buf = x
    for bit in bits:
        half = buf.shape[0] // 2
        mine = (me >> bit) & 1
        keep = lax.dynamic_slice_in_dim(buf, mine * half, half, 0)
        send = lax.dynamic_slice_in_dim(buf, (1 - mine) * half, half, 0)
        buf = keep + lax.ppermute(send, axis, xor_pairs(n, bit))
    return buf[0]


def position(d, bits):
    k = len(bits)
    return sum(((d >> bit) & 1) << (k - 1 - t) for t, bit in enumerate(bits))


def index_bits(n):
    return list(range(n.bit_length() - 1))


def project_kernel(p_ref, w_ref, l_ref, gm_ref, pt_ref, *, n_seq, orders):
    rows = p_ref.shape[0]
    width = p_ref.shape[1]
    per_block = width // 16
    half = C // len(orders)
    for i in range(rows):
        prod = lax.dot_general(
            w_ref[...], p_ref[i], (((1,), (1,)), ((), ())), preferred_element_type=jnp.float32
        )
        grad = (prod / n_seq).astype(jnp.bfloat16)
        for e in range(C):
            gm_ref[e, i * C:(i + 1) * C, :] = grad[e * C:(e + 1) * C, :]
    first = pl.program_id(0) * per_block
    for e in range(C):
        part = lax.dot_general(
            gm_ref[e], l_ref[...], (((0,), (1,)), ((), ())), preferred_element_type=jnp.float32
        )
        part = part.reshape(per_block, 16, part.shape[1])
        h = e // half
        for local in range(per_block):
            pt_ref[h, position(first + local, orders[h]), e % half] = part[local]


def left_kernel(gm_ref, rt_ref, out_ref):
    @pl.when(pl.program_id(0) == 0)
    def _():
        out_ref[...] = jnp.zeros_like(out_ref)

    width = gm_ref.shape[2]
    acc = out_ref[...]
    for e in range(C):
        right_e = rt_ref[:, e, :, :].reshape(width, rt_ref.shape[3])
        acc = acc + jnp.dot(gm_ref[e], right_e, preferred_element_type=jnp.float32)
    out_ref[...] = acc


def per_device(left_proj, right_proj, pair_cot, out_weight):
    n_seq = left_proj.shape[0]
    own_rows = pair_cot.shape[0]
    total = pair_cot.shape[1]
    p_size = pair_cot.shape[2]
    n = lax.axis_size("row")
    bits = index_bits(n)
    block = math.gcd(total, 256)
    steps = total // block
    per_dev = right_proj.shape[1] // C

    right_t = right_proj.reshape(n_seq, per_dev, C).transpose(2, 1, 0)
    swapped = bits[:1] + bits[1:3][::-1] + bits[3:]
    orders = (tuple(bits), tuple(swapped))
    half = C // len(orders)
    early = 2
    gathers = [(right_t[h * half:(h + 1) * half][None], []) for h in range(len(orders))]
    for h in range(len(orders)):
        for bit in orders[h][::-1][:early]:
            gathers[h] = gather_step(gathers[h], "row", n, bit)

    weight_ec = out_weight.reshape(C, C, p_size).transpose(1, 0, 2).reshape(C * C, p_size)

    grad_m, part_t = pl.pallas_call(
        functools.partial(project_kernel, n_seq=n_seq, orders=orders),
        grid=(steps,),
        in_specs=[
            pl.BlockSpec((own_rows, block, p_size), lambda b: (0, b, 0)),
            pl.BlockSpec((C * C, p_size), lambda b: (0, 0)),
            pl.BlockSpec((n_seq, own_rows * C), lambda b: (0, 0)),
        ],
        out_specs=[
            pl.BlockSpec((C, own_rows * C, block), lambda b: (0, 0, b)),
            pl.BlockSpec((len(orders), total // 16, half, 16, n_seq), lambda b: (0, 0, 0, 0, 0)),
        ],
        out_shape=[
            jax.ShapeDtypeStruct((C, own_rows * C, total), jnp.bfloat16),
            jax.ShapeDtypeStruct((len(orders), total // 16, half, 16, n_seq), jnp.float32),
        ],
        compiler_params=pltpu.CompilerParams(vmem_limit_bytes=56 * 1024 * 1024),
        cost_estimate=pl.CostEstimate(
            flops=2 * own_rows * total * C * C * (p_size + n_seq),
            transcendentals=0,
            bytes_accessed=2 * own_rows * total * (p_size + C * C) + 4 * total * C * n_seq,
        ),
    )(pair_cot, weight_ec, left_proj)

    scatters = [scatter_step(part_t[h], "row", n, orders[h][0]) for h in range(len(orders))]
    bufs = [g[0] for g in gathers]
    scatters, bufs = lax.optimization_barrier((scatters, bufs))
    gathers = [(bufs[h], gathers[h][1]) for h in range(len(orders))]
    for h in range(len(orders)):
        for bit in orders[h][::-1][early:]:
            gathers[h] = gather_step(gathers[h], "row", n, bit)
    right_blocks = jnp.concatenate(
        [gather_finish(gathers[h], n, right_t[:half].shape) for h in range(len(orders))], 1
    )
    for h in range(len(orders)):
        for bit in orders[h][1:]:
            scatters[h] = scatter_step(scatters[h], "row", n, bit)
    summed = jnp.concatenate([scatters[h][0] for h in range(len(orders))], 0)
    grad_right = summed.transpose(2, 1, 0).reshape(n_seq, per_dev * C).astype(jnp.bfloat16)

    left_t = pl.pallas_call(
        left_kernel,
        grid=(steps,),
        in_specs=[
            pl.BlockSpec((C, own_rows * C, block), lambda b: (0, 0, b)),
            pl.BlockSpec((block // 16, C, 16, n_seq), lambda b: (b, 0, 0, 0)),
        ],
        out_specs=pl.BlockSpec((own_rows * C, n_seq), lambda b: (0, 0)),
        out_shape=jax.ShapeDtypeStruct((own_rows * C, n_seq), jnp.float32),
        compiler_params=pltpu.CompilerParams(vmem_limit_bytes=56 * 1024 * 1024),
        cost_estimate=pl.CostEstimate(
            flops=2 * own_rows * total * C * C * n_seq,
            transcendentals=0,
            bytes_accessed=2 * own_rows * total * C * C + 2 * total * C * n_seq,
        ),
    )(grad_m, right_blocks)
    grad_left = left_t.T.astype(jnp.bfloat16)
    return (grad_left, grad_right)


def solution(mesh):
    return jax.shard_map(
        per_device,
        mesh=mesh,
        in_specs=(P("groups", "row"), P("groups", "row"), P(("groups", "row"), None, None), P()),
        out_specs=(P("groups", "row"), P("groups", "row")),
        check_vma=False,
    )
```

```python
import functools
import math

import jax
import jax.numpy as jnp
from jax import lax
from jax.experimental import pallas as pl
from jax.experimental.pallas import tpu as pltpu
from jax.sharding import PartitionSpec as P

C = 32


def xor_pairs(n, bit):
    return [(i, i ^ (1 << bit)) for i in range(n)]


def gather_blocks(x, axis, n, bits):
    me = lax.axis_index(axis)
    buf = x[None]
    done = []
    for bit in bits:
        other = lax.ppermute(buf, axis, xor_pairs(n, bit))
        mine = (me >> bit) & 1
        low = jnp.where(mine == 0, buf, other)
        high = jnp.where(mine == 0, other, buf)
        buf = jnp.concatenate([low, high], 0)
        done = [bit] + done
    k = len(done)
    buf = buf.reshape((2,) * k + x.shape)
    order = sorted(range(k), key=lambda t: -done[t])
    buf = buf.transpose(order + list(range(k, k + x.ndim)))
    return buf.reshape((n,) + x.shape)


def scatter_sum(x, axis, n, bits):
    me = lax.axis_index(axis)
    k = n.bit_length() - 1
    buf = x.reshape((2,) * k + x.shape[1:])
    left = list(range(k - 1, -1, -1))
    for bit in bits:
        t = left.index(bit)
        mine = (me >> bit) & 1
        moved = jnp.moveaxis(buf, t, 0)
        keep = lax.dynamic_index_in_dim(moved, mine, 0, keepdims=False)
        send = lax.dynamic_index_in_dim(moved, 1 - mine, 0, keepdims=False)
        buf = keep + lax.ppermute(send, axis, xor_pairs(n, bit))
        left.pop(t)
    return buf


def gather_step(state, axis, n, bit):
    buf, done = state
    me = lax.axis_index(axis)
    other = lax.ppermute(buf, axis, xor_pairs(n, bit))
    mine = (me >> bit) & 1
    low = jnp.where(mine == 0, buf, other)
    high = jnp.where(mine == 0, other, buf)
    return jnp.concatenate([low, high], 0), [bit] + done


def gather_finish(state, n, shape):
    buf, done = state
    k = len(done)
    buf = buf.reshape((2,) * k + shape)
    order = sorted(range(k), key=lambda t: -done[t])
    buf = buf.transpose(order + list(range(k, k + len(shape))))
    return buf.reshape((n,) + shape)


def scatter_step(buf, axis, n, bit):
    me = lax.axis_index(axis)
    half = buf.shape[0] // 2
    mine = (me >> bit) & 1
    keep = lax.dynamic_slice_in_dim(buf, mine * half, half, 0)
    send = lax.dynamic_slice_in_dim(buf, (1 - mine) * half, half, 0)
    return keep + lax.ppermute(send, axis, xor_pairs(n, bit))


def scatter_sum_ordered(x, axis, bits):
    me = lax.axis_index(axis)
    n = x.shape[0]
    buf = x
    for bit in bits:
        half = buf.shape[0] // 2
        mine = (me >> bit) & 1
        keep = lax.dynamic_slice_in_dim(buf, mine * half, half, 0)
        send = lax.dynamic_slice_in_dim(buf, (1 - mine) * half, half, 0)
        buf = keep + lax.ppermute(send, axis, xor_pairs(n, bit))
    return buf[0]


def position(d, bits):
    k = len(bits)
    return sum(((d >> bit) & 1) << (k - 1 - t) for t, bit in enumerate(bits))


def index_bits(n):
    return list(range(n.bit_length() - 1))


def project_kernel(p_ref, w_ref, l_ref, gm_ref, *pt_refs, n_seq, orders):
    rows = p_ref.shape[0]
    width = p_ref.shape[1]
    per_block = width // 16
    half = C // len(orders)
    for i in range(rows):
        prod = lax.dot_general(
            w_ref[...], p_ref[i], (((1,), (1,)), ((), ())), preferred_element_type=jnp.float32
        )
        grad = (prod / n_seq).astype(jnp.bfloat16)
        for e in range(C):
            gm_ref[e, i * C:(i + 1) * C, :] = grad[e * C:(e + 1) * C, :]
    first = pl.program_id(0) * per_block
    for e in range(C):
        part = lax.dot_general(
            gm_ref[e], l_ref[...], (((0,), (1,)), ((), ())), preferred_element_type=jnp.float32
        )
        part = part.reshape(per_block, 16, part.shape[1])
        h = e // half
        for local in range(per_block):
            pt_refs[h][position(first + local, orders[h]), e % half] = part[local]


def left_kernel(gm_ref, rt_ref, out_ref):
    @pl.when(pl.program_id(0) == 0)
    def _():
        out_ref[...] = jnp.zeros_like(out_ref)

    width = gm_ref.shape[2]
    acc = out_ref[...]
    for e in range(gm_ref.shape[0]):
        right_e = rt_ref[:, e, :, :].reshape(width, rt_ref.shape[3])
        acc = acc + jnp.dot(gm_ref[e], right_e, preferred_element_type=jnp.float32)
    out_ref[...] = acc


def per_device(left_proj, right_proj, pair_cot, out_weight):
    n_seq = left_proj.shape[0]
    own_rows = pair_cot.shape[0]
    total = pair_cot.shape[1]
    p_size = pair_cot.shape[2]
    n = lax.axis_size("row")
    bits = index_bits(n)
    block = math.gcd(total, 256)
    steps = total // block
    per_dev = right_proj.shape[1] // C

    right_t = right_proj.reshape(n_seq, per_dev, C).transpose(2, 1, 0)
    swapped = bits[:1] + bits[1:3][::-1] + bits[3:]
    orders = (tuple(bits), tuple(swapped))
    half = C // len(orders)
    early = 2
    gathers = [(right_t[h * half:(h + 1) * half][None], []) for h in range(len(orders))]
    for h in range(len(orders)):
        for bit in orders[h][::-1][:early]:
            gathers[h] = gather_step(gathers[h], "row", n, bit)

    weight_ec = out_weight.reshape(C, C, p_size).transpose(1, 0, 2).reshape(C * C, p_size)

    grad_m, *part_t = pl.pallas_call(
        functools.partial(project_kernel, n_seq=n_seq, orders=orders),
        grid=(steps,),
        in_specs=[
            pl.BlockSpec((own_rows, block, p_size), lambda b: (0, b, 0)),
            pl.BlockSpec((C * C, p_size), lambda b: (0, 0)),
            pl.BlockSpec((n_seq, own_rows * C), lambda b: (0, 0)),
        ],
        out_specs=[
            pl.BlockSpec((C, own_rows * C, block), lambda b: (0, 0, b)),
        ]
        + [pl.BlockSpec((total // 16, half, 16, n_seq), lambda b: (0, 0, 0, 0))] * len(orders),
        out_shape=[
            jax.ShapeDtypeStruct((C, own_rows * C, total), jnp.bfloat16),
        ]
        + [jax.ShapeDtypeStruct((total // 16, half, 16, n_seq), jnp.float32)] * len(orders),
        compiler_params=pltpu.CompilerParams(vmem_limit_bytes=56 * 1024 * 1024),
        cost_estimate=pl.CostEstimate(
            flops=2 * own_rows * total * C * C * (p_size + n_seq),
            transcendentals=0,
            bytes_accessed=2 * own_rows * total * (p_size + C * C) + 4 * total * C * n_seq,
        ),
    )(pair_cot, weight_ec, left_proj)

    scatters = [scatter_step(part_t[h], "row", n, orders[h][0]) for h in range(len(orders))]
    bufs = [g[0] for g in gathers]
    scatters, bufs = lax.optimization_barrier((scatters, bufs))
    gathers = [(bufs[h], gathers[h][1]) for h in range(len(orders))]
    for h in range(len(orders)):
        for bit in orders[h][::-1][early:]:
            gathers[h] = gather_step(gathers[h], "row", n, bit)
    right_halves = [gather_finish(gathers[h], n, right_t[:half].shape) for h in range(len(orders))]
    for h in range(len(orders)):
        for bit in orders[h][1:]:
            scatters[h] = scatter_step(scatters[h], "row", n, bit)
    summed = jnp.concatenate([scatters[h][0] for h in range(len(orders))], 0)
    grad_right = summed.transpose(2, 1, 0).reshape(n_seq, per_dev * C).astype(jnp.bfloat16)

    left_t = None
    for h in range(len(orders)):
        piece = pl.pallas_call(
            left_kernel,
            grid=(steps,),
            in_specs=[
                pl.BlockSpec((half, own_rows * C, block), lambda b, h=h: (h, 0, b)),
                pl.BlockSpec((block // 16, half, 16, n_seq), lambda b: (b, 0, 0, 0)),
            ],
            out_specs=pl.BlockSpec((own_rows * C, n_seq), lambda b: (0, 0)),
            out_shape=jax.ShapeDtypeStruct((own_rows * C, n_seq), jnp.float32),
            compiler_params=pltpu.CompilerParams(vmem_limit_bytes=56 * 1024 * 1024),
            cost_estimate=pl.CostEstimate(
                flops=2 * own_rows * total * C * half * n_seq,
                transcendentals=0,
                bytes_accessed=2 * own_rows * total * C * half + 2 * total * half * n_seq,
            ),
        )(grad_m, right_halves[h])
        left_t = piece if left_t is None else left_t + piece
    grad_left = left_t.T.astype(jnp.bfloat16)
    return (grad_left, grad_right)


def solution(mesh):
    return jax.shard_map(
        per_device,
        mesh=mesh,
        in_specs=(P("groups", "row"), P("groups", "row"), P(("groups", "row"), None, None), P()),
        out_specs=(P("groups", "row"), P("groups", "row")),
        check_vma=False,
    )
```

```python
import functools
import math

import jax
import jax.numpy as jnp
from jax import lax
from jax.experimental import pallas as pl
from jax.experimental.pallas import tpu as pltpu
from jax.sharding import PartitionSpec as P

C = 32


def xor_pairs(n, bit):
    return [(i, i ^ (1 << bit)) for i in range(n)]


def gather_blocks(x, axis, n, bits):
    me = lax.axis_index(axis)
    buf = x[None]
    done = []
    for bit in bits:
        other = lax.ppermute(buf, axis, xor_pairs(n, bit))
        mine = (me >> bit) & 1
        low = jnp.where(mine == 0, buf, other)
        high = jnp.where(mine == 0, other, buf)
        buf = jnp.concatenate([low, high], 0)
        done = [bit] + done
    k = len(done)
    buf = buf.reshape((2,) * k + x.shape)
    order = sorted(range(k), key=lambda t: -done[t])
    buf = buf.transpose(order + list(range(k, k + x.ndim)))
    return buf.reshape((n,) + x.shape)


def scatter_sum(x, axis, n, bits):
    me = lax.axis_index(axis)
    k = n.bit_length() - 1
    buf = x.reshape((2,) * k + x.shape[1:])
    left = list(range(k - 1, -1, -1))
    for bit in bits:
        t = left.index(bit)
        mine = (me >> bit) & 1
        moved = jnp.moveaxis(buf, t, 0)
        keep = lax.dynamic_index_in_dim(moved, mine, 0, keepdims=False)
        send = lax.dynamic_index_in_dim(moved, 1 - mine, 0, keepdims=False)
        buf = keep + lax.ppermute(send, axis, xor_pairs(n, bit))
        left.pop(t)
    return buf


def gather_step(state, axis, n, bit):
    buf, done = state
    me = lax.axis_index(axis)
    other = lax.ppermute(buf, axis, xor_pairs(n, bit))
    mine = (me >> bit) & 1
    low = jnp.where(mine == 0, buf, other)
    high = jnp.where(mine == 0, other, buf)
    return jnp.concatenate([low, high], 0), [bit] + done


def gather_finish(state, n, shape):
    buf, done = state
    k = len(done)
    buf = buf.reshape((2,) * k + shape)
    order = sorted(range(k), key=lambda t: -done[t])
    buf = buf.transpose(order + list(range(k, k + len(shape))))
    return buf.reshape((n,) + shape)


def scatter_step(buf, axis, n, bit):
    me = lax.axis_index(axis)
    half = buf.shape[0] // 2
    mine = (me >> bit) & 1
    keep = lax.dynamic_slice_in_dim(buf, mine * half, half, 0)
    send = lax.dynamic_slice_in_dim(buf, (1 - mine) * half, half, 0)
    return keep + lax.ppermute(send, axis, xor_pairs(n, bit))


def scatter_sum_ordered(x, axis, bits):
    me = lax.axis_index(axis)
    n = x.shape[0]
    buf = x
    for bit in bits:
        half = buf.shape[0] // 2
        mine = (me >> bit) & 1
        keep = lax.dynamic_slice_in_dim(buf, mine * half, half, 0)
        send = lax.dynamic_slice_in_dim(buf, (1 - mine) * half, half, 0)
        buf = keep + lax.ppermute(send, axis, xor_pairs(n, bit))
    return buf[0]


def position(d, bits):
    k = len(bits)
    return sum(((d >> bit) & 1) << (k - 1 - t) for t, bit in enumerate(bits))


def index_bits(n):
    return list(range(n.bit_length() - 1))


def project_kernel(p_ref, w_ref, l_ref, gm_ref, *pt_refs, n_seq, orders):
    rows = p_ref.shape[0]
    width = p_ref.shape[1]
    per_block = width // 16
    half = C // len(orders)
    for i in range(rows):
        prod = lax.dot_general(
            w_ref[...], p_ref[i], (((1,), (1,)), ((), ())), preferred_element_type=jnp.float32
        )
        grad = (prod / n_seq).astype(jnp.bfloat16)
        for e in range(C):
            gm_ref[e, i * C:(i + 1) * C, :] = grad[e * C:(e + 1) * C, :]
    first = pl.program_id(0) * per_block
    for e in range(C):
        part = lax.dot_general(
            gm_ref[e], l_ref[...], (((0,), (1,)), ((), ())), preferred_element_type=jnp.float32
        )
        part = part.reshape(per_block, 16, part.shape[1])
        h = e // half
        for local in range(per_block):
            pt_refs[h][position(first + local, orders[h]), e % half] = part[local]


def left_kernel(gm_ref, rt_ref, out_ref):
    @pl.when(pl.program_id(0) == 0)
    def _():
        out_ref[...] = jnp.zeros_like(out_ref)

    width = gm_ref.shape[2]
    acc = out_ref[...]
    for e in range(gm_ref.shape[0]):
        right_e = rt_ref[:, e, :, :].reshape(width, rt_ref.shape[3])
        acc = acc + jnp.dot(gm_ref[e], right_e, preferred_element_type=jnp.float32)
    out_ref[...] = acc


def per_device(left_proj, right_proj, pair_cot, out_weight):
    n_seq = left_proj.shape[0]
    own_rows = pair_cot.shape[0]
    total = pair_cot.shape[1]
    p_size = pair_cot.shape[2]
    n = lax.axis_size("row")
    bits = index_bits(n)
    block = math.gcd(total, 256)
    steps = total // block
    per_dev = right_proj.shape[1] // C

    right_t = right_proj.reshape(n_seq, per_dev, C).transpose(2, 1, 0)
    swapped = bits[:1] + bits[1:3][::-1] + bits[3:]
    orders = (tuple(bits), tuple(swapped))
    half = C // len(orders)
    early = 1
    gathers = [(right_t[h * half:(h + 1) * half][None], []) for h in range(len(orders))]
    for h in range(len(orders)):
        for bit in orders[h][::-1][:early]:
            gathers[h] = gather_step(gathers[h], "row", n, bit)

    weight_ec = out_weight.reshape(C, C, p_size).transpose(1, 0, 2).reshape(C * C, p_size)

    grad_m, *part_t = pl.pallas_call(
        functools.partial(project_kernel, n_seq=n_seq, orders=orders),
        grid=(steps,),
        in_specs=[
            pl.BlockSpec((own_rows, block, p_size), lambda b: (0, b, 0)),
            pl.BlockSpec((C * C, p_size), lambda b: (0, 0)),
            pl.BlockSpec((n_seq, own_rows * C), lambda b: (0, 0)),
        ],
        out_specs=[
            pl.BlockSpec((C, own_rows * C, block), lambda b: (0, 0, b)),
        ]
        + [pl.BlockSpec((total // 16, half, 16, n_seq), lambda b: (0, 0, 0, 0))] * len(orders),
        out_shape=[
            jax.ShapeDtypeStruct((C, own_rows * C, total), jnp.bfloat16),
        ]
        + [jax.ShapeDtypeStruct((total // 16, half, 16, n_seq), jnp.float32)] * len(orders),
        compiler_params=pltpu.CompilerParams(vmem_limit_bytes=56 * 1024 * 1024),
        cost_estimate=pl.CostEstimate(
            flops=2 * own_rows * total * C * C * (p_size + n_seq),
            transcendentals=0,
            bytes_accessed=2 * own_rows * total * (p_size + C * C) + 4 * total * C * n_seq,
        ),
    )(pair_cot, weight_ec, left_proj)

    scatters = [scatter_step(part_t[h], "row", n, orders[h][0]) for h in range(len(orders))]
    bufs = [g[0] for g in gathers]
    scatters, bufs = lax.optimization_barrier((scatters, bufs))
    gathers = [(bufs[h], gathers[h][1]) for h in range(len(orders))]
    for h in range(len(orders)):
        for bit in orders[h][::-1][early:]:
            gathers[h] = gather_step(gathers[h], "row", n, bit)
    right_halves = [gather_finish(gathers[h], n, right_t[:half].shape) for h in range(len(orders))]
    for h in range(len(orders)):
        for bit in orders[h][1:]:
            scatters[h] = scatter_step(scatters[h], "row", n, bit)
    summed = jnp.concatenate([scatters[h][0] for h in range(len(orders))], 0)
    grad_right = summed.transpose(2, 1, 0).reshape(n_seq, per_dev * C).astype(jnp.bfloat16)

    left_t = None
    for h in range(len(orders)):
        piece = pl.pallas_call(
            left_kernel,
            grid=(steps,),
            in_specs=[
                pl.BlockSpec((half, own_rows * C, block), lambda b, h=h: (h, 0, b)),
                pl.BlockSpec((block // 16, half, 16, n_seq), lambda b: (b, 0, 0, 0)),
            ],
            out_specs=pl.BlockSpec((own_rows * C, n_seq), lambda b: (0, 0)),
            out_shape=jax.ShapeDtypeStruct((own_rows * C, n_seq), jnp.float32),
            compiler_params=pltpu.CompilerParams(vmem_limit_bytes=56 * 1024 * 1024),
            cost_estimate=pl.CostEstimate(
                flops=2 * own_rows * total * C * half * n_seq,
                transcendentals=0,
                bytes_accessed=2 * own_rows * total * C * half + 2 * total * half * n_seq,
            ),
        )(grad_m, right_halves[h])
        left_t = piece if left_t is None else left_t + piece
    grad_left = left_t.T.astype(jnp.bfloat16)
    return (grad_left, grad_right)


def solution(mesh):
    return jax.shard_map(
        per_device,
        mesh=mesh,
        in_specs=(P("groups", "row"), P("groups", "row"), P(("groups", "row"), None, None), P()),
        out_specs=(P("groups", "row"), P("groups", "row")),
        check_vma=False,
    )
```

```python
import functools
import math

import jax
import jax.numpy as jnp
from jax import lax
from jax.experimental import pallas as pl
from jax.experimental.pallas import tpu as pltpu
from jax.sharding import PartitionSpec as P

C = 32


def xor_pairs(n, bit):
    return [(i, i ^ (1 << bit)) for i in range(n)]


def gather_blocks(x, axis, n, bits):
    me = lax.axis_index(axis)
    buf = x[None]
    done = []
    for bit in bits:
        other = lax.ppermute(buf, axis, xor_pairs(n, bit))
        mine = (me >> bit) & 1
        low = jnp.where(mine == 0, buf, other)
        high = jnp.where(mine == 0, other, buf)
        buf = jnp.concatenate([low, high], 0)
        done = [bit] + done
    k = len(done)
    buf = buf.reshape((2,) * k + x.shape)
    order = sorted(range(k), key=lambda t: -done[t])
    buf = buf.transpose(order + list(range(k, k + x.ndim)))
    return buf.reshape((n,) + x.shape)


def scatter_sum(x, axis, n, bits):
    me = lax.axis_index(axis)
    k = n.bit_length() - 1
    buf = x.reshape((2,) * k + x.shape[1:])
    left = list(range(k - 1, -1, -1))
    for bit in bits:
        t = left.index(bit)
        mine = (me >> bit) & 1
        moved = jnp.moveaxis(buf, t, 0)
        keep = lax.dynamic_index_in_dim(moved, mine, 0, keepdims=False)
        send = lax.dynamic_index_in_dim(moved, 1 - mine, 0, keepdims=False)
        buf = keep + lax.ppermute(send, axis, xor_pairs(n, bit))
        left.pop(t)
    return buf


def gather_step(state, axis, n, bit):
    buf, done = state
    me = lax.axis_index(axis)
    other = lax.ppermute(buf, axis, xor_pairs(n, bit))
    mine = (me >> bit) & 1
    low = jnp.where(mine == 0, buf, other)
    high = jnp.where(mine == 0, other, buf)
    return jnp.concatenate([low, high], 0), [bit] + done


def gather_finish(state, n, shape):
    buf, done = state
    k = len(done)
    buf = buf.reshape((2,) * k + shape)
    order = sorted(range(k), key=lambda t: -done[t])
    buf = buf.transpose(order + list(range(k, k + len(shape))))
    return buf.reshape((n,) + shape)


def scatter_step(buf, axis, n, bit):
    half = buf.shape[0] // 2
    return buf[:half] + lax.ppermute(buf[half:], axis, xor_pairs(n, bit))


def scatter_sum_ordered(x, axis, bits):
    me = lax.axis_index(axis)
    n = x.shape[0]
    buf = x
    for bit in bits:
        half = buf.shape[0] // 2
        mine = (me >> bit) & 1
        keep = lax.dynamic_slice_in_dim(buf, mine * half, half, 0)
        send = lax.dynamic_slice_in_dim(buf, (1 - mine) * half, half, 0)
        buf = keep + lax.ppermute(send, axis, xor_pairs(n, bit))
    return buf[0]


def position(d, bits):
    k = len(bits)
    return sum(((d >> bit) & 1) << (k - 1 - t) for t, bit in enumerate(bits))


def index_bits(n):
    return list(range(n.bit_length() - 1))


def project_kernel(me_ref, p_ref, w_ref, l_ref, gm_ref, *pt_refs, n_seq, orders):
    rows = p_ref.shape[0]
    width = p_ref.shape[1]
    per_block = width // 16
    half = C // len(orders)
    for i in range(rows):
        prod = lax.dot_general(
            w_ref[...], p_ref[i], (((1,), (1,)), ((), ())), preferred_element_type=jnp.float32
        )
        grad = (prod / n_seq).astype(jnp.bfloat16)
        for e in range(C):
            gm_ref[e, i * C:(i + 1) * C, :] = grad[e * C:(e + 1) * C, :]
    first = pl.program_id(0) * per_block
    me = me_ref[0]
    for e in range(C):
        part = lax.dot_general(
            gm_ref[e], l_ref[...], (((0,), (1,)), ((), ())), preferred_element_type=jnp.float32
        )
        part = part.reshape(per_block, 16, part.shape[1])
        h = e // half
        for local in range(per_block):
            pt_refs[h][position((first + local) ^ me, orders[h]), e % half] = part[local]


def left_kernel(gm_ref, rt_ref, out_ref):
    @pl.when(pl.program_id(0) == 0)
    def _():
        out_ref[...] = jnp.zeros_like(out_ref)

    width = gm_ref.shape[2]
    acc = out_ref[...]
    for e in range(gm_ref.shape[0]):
        right_e = rt_ref[:, e, :, :].reshape(width, rt_ref.shape[3])
        acc = acc + jnp.dot(gm_ref[e], right_e, preferred_element_type=jnp.float32)
    out_ref[...] = acc


def per_device(left_proj, right_proj, pair_cot, out_weight):
    n_seq = left_proj.shape[0]
    own_rows = pair_cot.shape[0]
    total = pair_cot.shape[1]
    p_size = pair_cot.shape[2]
    n = lax.axis_size("row")
    bits = index_bits(n)
    block = math.gcd(total, 256)
    steps = total // block
    per_dev = right_proj.shape[1] // C

    right_t = right_proj.reshape(n_seq, per_dev, C).transpose(2, 1, 0)
    swapped = bits[:1] + bits[1:3][::-1] + bits[3:]
    orders = (tuple(bits), tuple(swapped))
    half = C // len(orders)
    early = 2
    gathers = [(right_t[h * half:(h + 1) * half][None], []) for h in range(len(orders))]
    for h in range(len(orders)):
        for bit in orders[h][::-1][:early]:
            gathers[h] = gather_step(gathers[h], "row", n, bit)

    weight_ec = out_weight.reshape(C, C, p_size).transpose(1, 0, 2).reshape(C * C, p_size)

    grad_m, *part_t = pl.pallas_call(
        functools.partial(project_kernel, n_seq=n_seq, orders=orders),
        grid=(steps,),
        in_specs=[
            pl.BlockSpec(memory_space=pltpu.SMEM),
            pl.BlockSpec((own_rows, block, p_size), lambda b: (0, b, 0)),
            pl.BlockSpec((C * C, p_size), lambda b: (0, 0)),
            pl.BlockSpec((n_seq, own_rows * C), lambda b: (0, 0)),
        ],
        out_specs=[
            pl.BlockSpec((C, own_rows * C, block), lambda b: (0, 0, b)),
        ]
        + [pl.BlockSpec((total // 16, half, 16, n_seq), lambda b: (0, 0, 0, 0))] * len(orders),
        out_shape=[
            jax.ShapeDtypeStruct((C, own_rows * C, total), jnp.bfloat16),
        ]
        + [jax.ShapeDtypeStruct((total // 16, half, 16, n_seq), jnp.float32)] * len(orders),
        compiler_params=pltpu.CompilerParams(vmem_limit_bytes=56 * 1024 * 1024),
        cost_estimate=pl.CostEstimate(
            flops=2 * own_rows * total * C * C * (p_size + n_seq),
            transcendentals=0,
            bytes_accessed=2 * own_rows * total * (p_size + C * C) + 4 * total * C * n_seq,
        ),
    )(lax.axis_index("row").astype(jnp.int32).reshape(1), pair_cot, weight_ec, left_proj)

    scatters = [scatter_step(part_t[h], "row", n, orders[h][0]) for h in range(len(orders))]
    bufs = [g[0] for g in gathers]
    scatters, bufs = lax.optimization_barrier((scatters, bufs))
    gathers = [(bufs[h], gathers[h][1]) for h in range(len(orders))]
    for h in range(len(orders)):
        for bit in orders[h][::-1][early:]:
            gathers[h] = gather_step(gathers[h], "row", n, bit)
    right_halves = [gather_finish(gathers[h], n, right_t[:half].shape) for h in range(len(orders))]
    for h in range(len(orders)):
        for bit in orders[h][1:]:
            scatters[h] = scatter_step(scatters[h], "row", n, bit)
    summed = jnp.concatenate([scatters[h][0] for h in range(len(orders))], 0)
    grad_right = summed.transpose(2, 1, 0).reshape(n_seq, per_dev * C).astype(jnp.bfloat16)

    left_t = None
    for h in range(len(orders)):
        piece = pl.pallas_call(
            left_kernel,
            grid=(steps,),
            in_specs=[
                pl.BlockSpec((half, own_rows * C, block), lambda b, h=h: (h, 0, b)),
                pl.BlockSpec((block // 16, half, 16, n_seq), lambda b: (b, 0, 0, 0)),
            ],
            out_specs=pl.BlockSpec((own_rows * C, n_seq), lambda b: (0, 0)),
            out_shape=jax.ShapeDtypeStruct((own_rows * C, n_seq), jnp.float32),
            compiler_params=pltpu.CompilerParams(vmem_limit_bytes=56 * 1024 * 1024),
            cost_estimate=pl.CostEstimate(
                flops=2 * own_rows * total * C * half * n_seq,
                transcendentals=0,
                bytes_accessed=2 * own_rows * total * C * half + 2 * total * half * n_seq,
            ),
        )(grad_m, right_halves[h])
        left_t = piece if left_t is None else left_t + piece
    grad_left = left_t.T.astype(jnp.bfloat16)
    return (grad_left, grad_right)


def solution(mesh):
    return jax.shard_map(
        per_device,
        mesh=mesh,
        in_specs=(P("groups", "row"), P("groups", "row"), P(("groups", "row"), None, None), P()),
        out_specs=(P("groups", "row"), P("groups", "row")),
        check_vma=False,
    )
```

```python
import functools
import math

import jax
import jax.numpy as jnp
from jax import lax
from jax.experimental import pallas as pl
from jax.experimental.pallas import tpu as pltpu
from jax.sharding import PartitionSpec as P

C = 32


def xor_pairs(n, bit):
    return [(i, i ^ (1 << bit)) for i in range(n)]


def gather_blocks(x, axis, n, bits):
    me = lax.axis_index(axis)
    buf = x[None]
    done = []
    for bit in bits:
        other = lax.ppermute(buf, axis, xor_pairs(n, bit))
        mine = (me >> bit) & 1
        low = jnp.where(mine == 0, buf, other)
        high = jnp.where(mine == 0, other, buf)
        buf = jnp.concatenate([low, high], 0)
        done = [bit] + done
    k = len(done)
    buf = buf.reshape((2,) * k + x.shape)
    order = sorted(range(k), key=lambda t: -done[t])
    buf = buf.transpose(order + list(range(k, k + x.ndim)))
    return buf.reshape((n,) + x.shape)


def scatter_sum(x, axis, n, bits):
    me = lax.axis_index(axis)
    k = n.bit_length() - 1
    buf = x.reshape((2,) * k + x.shape[1:])
    left = list(range(k - 1, -1, -1))
    for bit in bits:
        t = left.index(bit)
        mine = (me >> bit) & 1
        moved = jnp.moveaxis(buf, t, 0)
        keep = lax.dynamic_index_in_dim(moved, mine, 0, keepdims=False)
        send = lax.dynamic_index_in_dim(moved, 1 - mine, 0, keepdims=False)
        buf = keep + lax.ppermute(send, axis, xor_pairs(n, bit))
        left.pop(t)
    return buf


def gather_step(state, axis, n, bit):
    buf, done = state
    me = lax.axis_index(axis)
    other = lax.ppermute(buf, axis, xor_pairs(n, bit))
    mine = (me >> bit) & 1
    low = jnp.where(mine == 0, buf, other)
    high = jnp.where(mine == 0, other, buf)
    return jnp.concatenate([low, high], 0), [bit] + done


def gather_finish(state, n, shape):
    buf, done = state
    k = len(done)
    buf = buf.reshape((2,) * k + shape)
    order = sorted(range(k), key=lambda t: -done[t])
    buf = buf.transpose(order + list(range(k, k + len(shape))))
    return buf.reshape((n,) + shape)


def scatter_step(buf, axis, n, bit):
    me = lax.axis_index(axis)
    half = buf.shape[0] // 2
    mine = (me >> bit) & 1
    keep = lax.dynamic_slice_in_dim(buf, mine * half, half, 0)
    send = lax.dynamic_slice_in_dim(buf, (1 - mine) * half, half, 0)
    return keep + lax.ppermute(send, axis, xor_pairs(n, bit))


def scatter_sum_ordered(x, axis, bits):
    me = lax.axis_index(axis)
    n = x.shape[0]
    buf = x
    for bit in bits:
        half = buf.shape[0] // 2
        mine = (me >> bit) & 1
        keep = lax.dynamic_slice_in_dim(buf, mine * half, half, 0)
        send = lax.dynamic_slice_in_dim(buf, (1 - mine) * half, half, 0)
        buf = keep + lax.ppermute(send, axis, xor_pairs(n, bit))
    return buf[0]


def position(d, bits):
    k = len(bits)
    return sum(((d >> bit) & 1) << (k - 1 - t) for t, bit in enumerate(bits))


def index_bits(n):
    return list(range(n.bit_length() - 1))


def project_kernel(p_ref, w_ref, l_ref, gm_ref, *pt_refs, n_seq, orders):
    rows = p_ref.shape[0]
    width = p_ref.shape[1]
    per_block = width // 16
    half = C // len(orders)
    for i in range(rows):
        prod = lax.dot_general(
            w_ref[...], p_ref[i], (((1,), (1,)), ((), ())), preferred_element_type=jnp.float32
        )
        grad = (prod / n_seq).astype(jnp.bfloat16)
        for e in range(C):
            gm_ref[e, i * C:(i + 1) * C, :] = grad[e * C:(e + 1) * C, :]
    first = pl.program_id(0) * per_block
    for e in range(C):
        part = lax.dot_general(
            gm_ref[e], l_ref[...], (((0,), (1,)), ((), ())), preferred_element_type=jnp.float32
        )
        part = part.reshape(per_block, 16, part.shape[1])
        h = e // half
        for local in range(per_block):
            pt_refs[h][position(first + local, orders[h]), e % half] = part[local]


def left_kernel(gm_ref, rt_ref, out_ref):
    @pl.when(pl.program_id(0) == 0)
    def _():
        out_ref[...] = jnp.zeros_like(out_ref)

    width = gm_ref.shape[2]
    acc = out_ref[...]
    for e in range(gm_ref.shape[0]):
        right_e = rt_ref[:, e, :, :].reshape(width, rt_ref.shape[3])
        acc = acc + jnp.dot(gm_ref[e], right_e, preferred_element_type=jnp.float32)
    out_ref[...] = acc


def per_device(left_proj, right_proj, pair_cot, out_weight):
    n_seq = left_proj.shape[0]
    own_rows = pair_cot.shape[0]
    total = pair_cot.shape[1]
    p_size = pair_cot.shape[2]
    n = lax.axis_size("row")
    bits = index_bits(n)
    block = math.gcd(total, 256)
    steps = total // block
    per_dev = right_proj.shape[1] // C

    right_t = right_proj.reshape(n_seq, per_dev, C).transpose(2, 1, 0)
    swapped = bits[:1] + bits[1:3][::-1] + bits[3:]
    orders = (tuple(bits), tuple(swapped))
    half = C // len(orders)
    early = 2
    gathers = [(right_t[h * half:(h + 1) * half][None], []) for h in range(len(orders))]
    for h in range(len(orders)):
        for bit in orders[h][::-1][:early]:
            gathers[h] = gather_step(gathers[h], "row", n, bit)

    weight_ec = out_weight.reshape(C, C, p_size).transpose(1, 0, 2).reshape(C * C, p_size)

    grad_m, *part_t = pl.pallas_call(
        functools.partial(project_kernel, n_seq=n_seq, orders=orders),
        grid=(steps,),
        in_specs=[
            pl.BlockSpec((own_rows, block, p_size), lambda b: (0, b, 0)),
            pl.BlockSpec((C * C, p_size), lambda b: (0, 0)),
            pl.BlockSpec((n_seq, own_rows * C), lambda b: (0, 0)),
        ],
        out_specs=[
            pl.BlockSpec((C, own_rows * C, block), lambda b: (0, 0, b)),
        ]
        + [pl.BlockSpec((total // 16, half, 16, n_seq), lambda b: (0, 0, 0, 0))] * len(orders),
        out_shape=[
            jax.ShapeDtypeStruct((C, own_rows * C, total), jnp.bfloat16),
        ]
        + [jax.ShapeDtypeStruct((total // 16, half, 16, n_seq), jnp.float32)] * len(orders),
        compiler_params=pltpu.CompilerParams(vmem_limit_bytes=56 * 1024 * 1024),
        cost_estimate=pl.CostEstimate(
            flops=2 * own_rows * total * C * C * (p_size + n_seq),
            transcendentals=0,
            bytes_accessed=2 * own_rows * total * (p_size + C * C) + 4 * total * C * n_seq,
        ),
    )(pair_cot, weight_ec, left_proj)

    scatters = [scatter_step(part_t[h], "row", n, orders[h][0]) for h in range(len(orders))]
    bufs = [g[0] for g in gathers]
    scatters, bufs = lax.optimization_barrier((scatters, bufs))
    gathers = [(bufs[h], gathers[h][1]) for h in range(len(orders))]
    for h in range(len(orders)):
        for bit in orders[h][::-1][early:]:
            gathers[h] = gather_step(gathers[h], "row", n, bit)
    right_blocks = jnp.concatenate(
        [gather_finish(gathers[h], n, right_t[:half].shape) for h in range(len(orders))], 1
    )
    for h in range(len(orders)):
        for bit in orders[h][1:]:
            scatters[h] = scatter_step(scatters[h], "row", n, bit)
    summed = jnp.concatenate([scatters[h][0] for h in range(len(orders))], 0)
    grad_right = summed.transpose(2, 1, 0).reshape(n_seq, per_dev * C).astype(jnp.bfloat16)

    left_t = pl.pallas_call(
        left_kernel,
        grid=(steps,),
        in_specs=[
            pl.BlockSpec((C, own_rows * C, block), lambda b: (0, 0, b)),
            pl.BlockSpec((block // 16, C, 16, n_seq), lambda b: (b, 0, 0, 0)),
        ],
        out_specs=pl.BlockSpec((own_rows * C, n_seq), lambda b: (0, 0)),
        out_shape=jax.ShapeDtypeStruct((own_rows * C, n_seq), jnp.float32),
        compiler_params=pltpu.CompilerParams(vmem_limit_bytes=56 * 1024 * 1024),
        cost_estimate=pl.CostEstimate(
            flops=2 * own_rows * total * C * C * n_seq,
            transcendentals=0,
            bytes_accessed=2 * own_rows * total * C * C + 2 * total * C * n_seq,
        ),
    )(grad_m, right_blocks)
    grad_left = left_t.T.astype(jnp.bfloat16)
    return (grad_left, grad_right)


def solution(mesh):
    return jax.shard_map(
        per_device,
        mesh=mesh,
        in_specs=(P("groups", "row"), P("groups", "row"), P(("groups", "row"), None, None), P()),
        out_specs=(P("groups", "row"), P("groups", "row")),
        check_vma=False,
    )
```

```python
import functools
import math

import jax
import jax.numpy as jnp
from jax import lax
from jax.experimental import pallas as pl
from jax.experimental.pallas import tpu as pltpu
from jax.sharding import PartitionSpec as P

C = 32


def xor_pairs(n, bit):
    return [(i, i ^ (1 << bit)) for i in range(n)]


def gather_blocks(x, axis, n, bits):
    me = lax.axis_index(axis)
    buf = x[None]
    done = []
    for bit in bits:
        other = lax.ppermute(buf, axis, xor_pairs(n, bit))
        mine = (me >> bit) & 1
        low = jnp.where(mine == 0, buf, other)
        high = jnp.where(mine == 0, other, buf)
        buf = jnp.concatenate([low, high], 0)
        done = [bit] + done
    k = len(done)
    buf = buf.reshape((2,) * k + x.shape)
    order = sorted(range(k), key=lambda t: -done[t])
    buf = buf.transpose(order + list(range(k, k + x.ndim)))
    return buf.reshape((n,) + x.shape)


def scatter_sum(x, axis, n, bits):
    me = lax.axis_index(axis)
    k = n.bit_length() - 1
    buf = x.reshape((2,) * k + x.shape[1:])
    left = list(range(k - 1, -1, -1))
    for bit in bits:
        t = left.index(bit)
        mine = (me >> bit) & 1
        moved = jnp.moveaxis(buf, t, 0)
        keep = lax.dynamic_index_in_dim(moved, mine, 0, keepdims=False)
        send = lax.dynamic_index_in_dim(moved, 1 - mine, 0, keepdims=False)
        buf = keep + lax.ppermute(send, axis, xor_pairs(n, bit))
        left.pop(t)
    return buf


def gather_step(state, axis, n, bit):
    buf, done = state
    me = lax.axis_index(axis)
    other = lax.ppermute(buf, axis, xor_pairs(n, bit))
    mine = (me >> bit) & 1
    low = jnp.where(mine == 0, buf, other)
    high = jnp.where(mine == 0, other, buf)
    return jnp.concatenate([low, high], 0), [bit] + done


def gather_finish(state, n, shape):
    buf, done = state
    k = len(done)
    buf = buf.reshape((2,) * k + shape)
    order = sorted(range(k), key=lambda t: -done[t])
    buf = buf.transpose(order + list(range(k, k + len(shape))))
    return buf.reshape((n,) + shape)


def scatter_step(buf, axis, n, bit):
    me = lax.axis_index(axis)
    half = buf.shape[0] // 2
    mine = (me >> bit) & 1
    keep = lax.dynamic_slice_in_dim(buf, mine * half, half, 0)
    send = lax.dynamic_slice_in_dim(buf, (1 - mine) * half, half, 0)
    return keep + lax.ppermute(send, axis, xor_pairs(n, bit))


def scatter_sum_ordered(x, axis, bits):
    me = lax.axis_index(axis)
    n = x.shape[0]
    buf = x
    for bit in bits:
        half = buf.shape[0] // 2
        mine = (me >> bit) & 1
        keep = lax.dynamic_slice_in_dim(buf, mine * half, half, 0)
        send = lax.dynamic_slice_in_dim(buf, (1 - mine) * half, half, 0)
        buf = keep + lax.ppermute(send, axis, xor_pairs(n, bit))
    return buf[0]


def position(d, bits):
    k = len(bits)
    return sum(((d >> bit) & 1) << (k - 1 - t) for t, bit in enumerate(bits))


def index_bits(n):
    return list(range(n.bit_length() - 1))


def project_kernel(p_ref, w_ref, l_ref, gm_ref, *pt_refs, n_seq, orders):
    rows = p_ref.shape[0]
    width = p_ref.shape[1]
    per_block = width // 16
    half = C // len(orders)
    for i in range(rows):
        prod = lax.dot_general(
            w_ref[...], p_ref[i], (((1,), (1,)), ((), ())), preferred_element_type=jnp.float32
        )
        grad = (prod / n_seq).astype(jnp.bfloat16)
        for e in range(C):
            gm_ref[e, i * C:(i + 1) * C, :] = grad[e * C:(e + 1) * C, :]
    first = pl.program_id(0) * per_block
    for e in range(C):
        part = lax.dot_general(
            gm_ref[e], l_ref[...], (((0,), (1,)), ((), ())), preferred_element_type=jnp.float32
        )
        part = part.reshape(per_block, 16, part.shape[1])
        h = e // half
        for local in range(per_block):
            pt_refs[h][position(first + local, orders[h]), e % half] = part[local]


def left_kernel(gm_ref, rt_ref, out_ref):
    @pl.when(pl.program_id(0) == 0)
    def _():
        out_ref[...] = jnp.zeros_like(out_ref)

    width = gm_ref.shape[2]
    acc = out_ref[...]
    for e in range(gm_ref.shape[0]):
        right_e = rt_ref[:, e, :, :].reshape(width, rt_ref.shape[3])
        acc = acc + jnp.dot(gm_ref[e], right_e, preferred_element_type=jnp.float32)
    out_ref[...] = acc


def per_device(left_proj, right_proj, pair_cot, out_weight):
    n_seq = left_proj.shape[0]
    own_rows = pair_cot.shape[0]
    total = pair_cot.shape[1]
    p_size = pair_cot.shape[2]
    n = lax.axis_size("row")
    bits = index_bits(n)
    block = math.gcd(total, 256)
    steps = total // block
    per_dev = right_proj.shape[1] // C

    right_t = right_proj.reshape(n_seq, per_dev, C).transpose(2, 1, 0)
    swapped = bits[:1] + bits[1:3][::-1] + bits[3:]
    orders = (tuple(bits), tuple(swapped))
    half = C // len(orders)
    early = 0
    gathers = [(right_t[h * half:(h + 1) * half][None], []) for h in range(len(orders))]
    for h in range(len(orders)):
        for bit in orders[h][::-1][:early]:
            gathers[h] = gather_step(gathers[h], "row", n, bit)

    weight_ec = out_weight.reshape(C, C, p_size).transpose(1, 0, 2).reshape(C * C, p_size)

    grad_m, *part_t = pl.pallas_call(
        functools.partial(project_kernel, n_seq=n_seq, orders=orders),
        grid=(steps,),
        in_specs=[
            pl.BlockSpec((own_rows, block, p_size), lambda b: (0, b, 0)),
            pl.BlockSpec((C * C, p_size), lambda b: (0, 0)),
            pl.BlockSpec((n_seq, own_rows * C), lambda b: (0, 0)),
        ],
        out_specs=[
            pl.BlockSpec((C, own_rows * C, block), lambda b: (0, 0, b)),
        ]
        + [pl.BlockSpec((total // 16, half, 16, n_seq), lambda b: (0, 0, 0, 0))] * len(orders),
        out_shape=[
            jax.ShapeDtypeStruct((C, own_rows * C, total), jnp.bfloat16),
        ]
        + [jax.ShapeDtypeStruct((total // 16, half, 16, n_seq), jnp.float32)] * len(orders),
        compiler_params=pltpu.CompilerParams(vmem_limit_bytes=56 * 1024 * 1024),
        cost_estimate=pl.CostEstimate(
            flops=2 * own_rows * total * C * C * (p_size + n_seq),
            transcendentals=0,
            bytes_accessed=2 * own_rows * total * (p_size + C * C) + 4 * total * C * n_seq,
        ),
    )(pair_cot, weight_ec, left_proj)

    scatters = [scatter_step(part_t[h], "row", n, orders[h][0]) for h in range(len(orders))]
    bufs = [g[0] for g in gathers]
    scatters, bufs = lax.optimization_barrier((scatters, bufs))
    gathers = [(bufs[h], gathers[h][1]) for h in range(len(orders))]
    for h in range(len(orders)):
        for bit in orders[h][::-1][early:]:
            gathers[h] = gather_step(gathers[h], "row", n, bit)
    right_blocks = jnp.concatenate(
        [gather_finish(gathers[h], n, right_t[:half].shape) for h in range(len(orders))], 1
    )
    for h in range(len(orders)):
        for bit in orders[h][1:]:
            scatters[h] = scatter_step(scatters[h], "row", n, bit)
    summed = jnp.concatenate([scatters[h][0] for h in range(len(orders))], 0)
    grad_right = summed.transpose(2, 1, 0).reshape(n_seq, per_dev * C).astype(jnp.bfloat16)

    left_t = pl.pallas_call(
        left_kernel,
        grid=(steps,),
        in_specs=[
            pl.BlockSpec((C, own_rows * C, block), lambda b: (0, 0, b)),
            pl.BlockSpec((block // 16, C, 16, n_seq), lambda b: (b, 0, 0, 0)),
        ],
        out_specs=pl.BlockSpec((own_rows * C, n_seq), lambda b: (0, 0)),
        out_shape=jax.ShapeDtypeStruct((own_rows * C, n_seq), jnp.float32),
        compiler_params=pltpu.CompilerParams(vmem_limit_bytes=56 * 1024 * 1024),
        cost_estimate=pl.CostEstimate(
            flops=2 * own_rows * total * C * C * n_seq,
            transcendentals=0,
            bytes_accessed=2 * own_rows * total * C * C + 2 * total * C * n_seq,
        ),
    )(grad_m, right_blocks)
    grad_left = left_t.T.astype(jnp.bfloat16)
    return (grad_left, grad_right)


def solution(mesh):
    return jax.shard_map(
        per_device,
        mesh=mesh,
        in_specs=(P("groups", "row"), P("groups", "row"), P(("groups", "row"), None, None), P()),
        out_specs=(P("groups", "row"), P("groups", "row")),
        check_vma=False,
    )
```

```python
import functools
import math

import jax
import jax.numpy as jnp
from jax import lax
from jax.experimental import pallas as pl
from jax.experimental.pallas import tpu as pltpu
from jax.sharding import PartitionSpec as P

C = 32


def xor_pairs(n, bit):
    return [(i, i ^ (1 << bit)) for i in range(n)]


def gather_blocks(x, axis, n, bits):
    me = lax.axis_index(axis)
    buf = x[None]
    done = []
    for bit in bits:
        other = lax.ppermute(buf, axis, xor_pairs(n, bit))
        mine = (me >> bit) & 1
        low = jnp.where(mine == 0, buf, other)
        high = jnp.where(mine == 0, other, buf)
        buf = jnp.concatenate([low, high], 0)
        done = [bit] + done
    k = len(done)
    buf = buf.reshape((2,) * k + x.shape)
    order = sorted(range(k), key=lambda t: -done[t])
    buf = buf.transpose(order + list(range(k, k + x.ndim)))
    return buf.reshape((n,) + x.shape)


def scatter_sum(x, axis, n, bits):
    me = lax.axis_index(axis)
    k = n.bit_length() - 1
    buf = x.reshape((2,) * k + x.shape[1:])
    left = list(range(k - 1, -1, -1))
    for bit in bits:
        t = left.index(bit)
        mine = (me >> bit) & 1
        moved = jnp.moveaxis(buf, t, 0)
        keep = lax.dynamic_index_in_dim(moved, mine, 0, keepdims=False)
        send = lax.dynamic_index_in_dim(moved, 1 - mine, 0, keepdims=False)
        buf = keep + lax.ppermute(send, axis, xor_pairs(n, bit))
        left.pop(t)
    return buf


def gather_step(state, axis, n, bit):
    buf, done = state
    me = lax.axis_index(axis)
    other = lax.ppermute(buf, axis, xor_pairs(n, bit))
    mine = (me >> bit) & 1
    low = jnp.where(mine == 0, buf, other)
    high = jnp.where(mine == 0, other, buf)
    return jnp.concatenate([low, high], 0), [bit] + done


def gather_finish(state, n, shape):
    buf, done = state
    k = len(done)
    buf = buf.reshape((2,) * k + shape)
    order = sorted(range(k), key=lambda t: -done[t])
    buf = buf.transpose(order + list(range(k, k + len(shape))))
    return buf.reshape((n,) + shape)


def scatter_step(buf, axis, n, bit):
    me = lax.axis_index(axis)
    half = buf.shape[0] // 2
    mine = (me >> bit) & 1
    keep = lax.dynamic_slice_in_dim(buf, mine * half, half, 0)
    send = lax.dynamic_slice_in_dim(buf, (1 - mine) * half, half, 0)
    return keep + lax.ppermute(send, axis, xor_pairs(n, bit))


def scatter_sum_ordered(x, axis, bits):
    me = lax.axis_index(axis)
    n = x.shape[0]
    buf = x
    for bit in bits:
        half = buf.shape[0] // 2
        mine = (me >> bit) & 1
        keep = lax.dynamic_slice_in_dim(buf, mine * half, half, 0)
        send = lax.dynamic_slice_in_dim(buf, (1 - mine) * half, half, 0)
        buf = keep + lax.ppermute(send, axis, xor_pairs(n, bit))
    return buf[0]


def position(d, bits):
    k = len(bits)
    return sum(((d >> bit) & 1) << (k - 1 - t) for t, bit in enumerate(bits))


def index_bits(n):
    return list(range(n.bit_length() - 1))


def project_kernel(p_ref, w_ref, l_ref, gm_ref, *pt_refs, n_seq, orders):
    rows = p_ref.shape[0]
    width = p_ref.shape[1]
    per_block = width // 16
    half = C // len(orders)
    for i in range(rows):
        prod = lax.dot_general(
            w_ref[...], p_ref[i], (((1,), (1,)), ((), ())), preferred_element_type=jnp.float32
        )
        grad = (prod / n_seq).astype(jnp.bfloat16)
        for e in range(C):
            gm_ref[e, i * C:(i + 1) * C, :] = grad[e * C:(e + 1) * C, :]
    first = pl.program_id(0) * per_block
    for e in range(C):
        part = lax.dot_general(
            gm_ref[e], l_ref[...], (((0,), (1,)), ((), ())), preferred_element_type=jnp.float32
        )
        part = part.reshape(per_block, 16, part.shape[1])
        h = e // half
        for local in range(per_block):
            pt_refs[h][position(first + local, orders[h]), e % half] = part[local]


def left_kernel(gm_ref, rt_ref, out_ref):
    @pl.when(pl.program_id(0) == 0)
    def _():
        out_ref[...] = jnp.zeros_like(out_ref)

    width = gm_ref.shape[2]
    acc = out_ref[...]
    for e in range(gm_ref.shape[0]):
        right_e = rt_ref[:, e, :, :].reshape(width, rt_ref.shape[3])
        acc = acc + jnp.dot(gm_ref[e], right_e, preferred_element_type=jnp.float32)
    out_ref[...] = acc


def per_device(left_proj, right_proj, pair_cot, out_weight):
    n_seq = left_proj.shape[0]
    own_rows = pair_cot.shape[0]
    total = pair_cot.shape[1]
    p_size = pair_cot.shape[2]
    n = lax.axis_size("row")
    bits = index_bits(n)
    block = math.gcd(total, 256)
    steps = total // block
    per_dev = right_proj.shape[1] // C

    right_t = right_proj.reshape(n_seq, per_dev, C).transpose(2, 1, 0)
    swapped = bits[:1] + bits[1:3][::-1] + bits[3:]
    orders = (tuple(bits), tuple(swapped))
    half = C // len(orders)
    early = 3
    gathers = [(right_t[h * half:(h + 1) * half][None], []) for h in range(len(orders))]
    for h in range(len(orders)):
        for bit in orders[h][::-1][:early]:
            gathers[h] = gather_step(gathers[h], "row", n, bit)

    weight_ec = out_weight.reshape(C, C, p_size).transpose(1, 0, 2).reshape(C * C, p_size)

    grad_m, *part_t = pl.pallas_call(
        functools.partial(project_kernel, n_seq=n_seq, orders=orders),
        grid=(steps,),
        in_specs=[
            pl.BlockSpec((own_rows, block, p_size), lambda b: (0, b, 0)),
            pl.BlockSpec((C * C, p_size), lambda b: (0, 0)),
            pl.BlockSpec((n_seq, own_rows * C), lambda b: (0, 0)),
        ],
        out_specs=[
            pl.BlockSpec((C, own_rows * C, block), lambda b: (0, 0, b)),
        ]
        + [pl.BlockSpec((total // 16, half, 16, n_seq), lambda b: (0, 0, 0, 0))] * len(orders),
        out_shape=[
            jax.ShapeDtypeStruct((C, own_rows * C, total), jnp.bfloat16),
        ]
        + [jax.ShapeDtypeStruct((total // 16, half, 16, n_seq), jnp.float32)] * len(orders),
        compiler_params=pltpu.CompilerParams(vmem_limit_bytes=56 * 1024 * 1024),
        cost_estimate=pl.CostEstimate(
            flops=2 * own_rows * total * C * C * (p_size + n_seq),
            transcendentals=0,
            bytes_accessed=2 * own_rows * total * (p_size + C * C) + 4 * total * C * n_seq,
        ),
    )(pair_cot, weight_ec, left_proj)

    scatters = [scatter_step(part_t[h], "row", n, orders[h][0]) for h in range(len(orders))]
    bufs = [g[0] for g in gathers]
    scatters, bufs = lax.optimization_barrier((scatters, bufs))
    gathers = [(bufs[h], gathers[h][1]) for h in range(len(orders))]
    for h in range(len(orders)):
        for bit in orders[h][::-1][early:]:
            gathers[h] = gather_step(gathers[h], "row", n, bit)
    right_blocks = jnp.concatenate(
        [gather_finish(gathers[h], n, right_t[:half].shape) for h in range(len(orders))], 1
    )
    for h in range(len(orders)):
        for bit in orders[h][1:]:
            scatters[h] = scatter_step(scatters[h], "row", n, bit)
    summed = jnp.concatenate([scatters[h][0] for h in range(len(orders))], 0)
    grad_right = summed.transpose(2, 1, 0).reshape(n_seq, per_dev * C).astype(jnp.bfloat16)

    left_t = pl.pallas_call(
        left_kernel,
        grid=(steps,),
        in_specs=[
            pl.BlockSpec((C, own_rows * C, block), lambda b: (0, 0, b)),
            pl.BlockSpec((block // 16, C, 16, n_seq), lambda b: (b, 0, 0, 0)),
        ],
        out_specs=pl.BlockSpec((own_rows * C, n_seq), lambda b: (0, 0)),
        out_shape=jax.ShapeDtypeStruct((own_rows * C, n_seq), jnp.float32),
        compiler_params=pltpu.CompilerParams(vmem_limit_bytes=56 * 1024 * 1024),
        cost_estimate=pl.CostEstimate(
            flops=2 * own_rows * total * C * C * n_seq,
            transcendentals=0,
            bytes_accessed=2 * own_rows * total * C * C + 2 * total * C * n_seq,
        ),
    )(grad_m, right_blocks)
    grad_left = left_t.T.astype(jnp.bfloat16)
    return (grad_left, grad_right)


def solution(mesh):
    return jax.shard_map(
        per_device,
        mesh=mesh,
        in_specs=(P("groups", "row"), P("groups", "row"), P(("groups", "row"), None, None), P()),
        out_specs=(P("groups", "row"), P("groups", "row")),
        check_vma=False,
    )
```

```python
import functools
import math

import jax
import jax.numpy as jnp
from jax import lax
from jax.experimental import pallas as pl
from jax.experimental.pallas import tpu as pltpu
from jax.sharding import PartitionSpec as P

C = 32


def xor_pairs(n, bit):
    return [(i, i ^ (1 << bit)) for i in range(n)]


def gather_blocks(x, axis, n, bits):
    me = lax.axis_index(axis)
    buf = x[None]
    done = []
    for bit in bits:
        other = lax.ppermute(buf, axis, xor_pairs(n, bit))
        mine = (me >> bit) & 1
        low = jnp.where(mine == 0, buf, other)
        high = jnp.where(mine == 0, other, buf)
        buf = jnp.concatenate([low, high], 0)
        done = [bit] + done
    k = len(done)
    buf = buf.reshape((2,) * k + x.shape)
    order = sorted(range(k), key=lambda t: -done[t])
    buf = buf.transpose(order + list(range(k, k + x.ndim)))
    return buf.reshape((n,) + x.shape)


def scatter_sum(x, axis, n, bits):
    me = lax.axis_index(axis)
    k = n.bit_length() - 1
    buf = x.reshape((2,) * k + x.shape[1:])
    left = list(range(k - 1, -1, -1))
    for bit in bits:
        t = left.index(bit)
        mine = (me >> bit) & 1
        moved = jnp.moveaxis(buf, t, 0)
        keep = lax.dynamic_index_in_dim(moved, mine, 0, keepdims=False)
        send = lax.dynamic_index_in_dim(moved, 1 - mine, 0, keepdims=False)
        buf = keep + lax.ppermute(send, axis, xor_pairs(n, bit))
        left.pop(t)
    return buf


def gather_step(state, axis, n, bit):
    buf, done = state
    me = lax.axis_index(axis)
    other = lax.ppermute(buf, axis, xor_pairs(n, bit))
    mine = (me >> bit) & 1
    low = jnp.where(mine == 0, buf, other)
    high = jnp.where(mine == 0, other, buf)
    return jnp.concatenate([low, high], 0), [bit] + done


def gather_finish(state, n, shape):
    buf, done = state
    k = len(done)
    buf = buf.reshape((2,) * k + shape)
    order = sorted(range(k), key=lambda t: -done[t])
    buf = buf.transpose(order + list(range(k, k + len(shape))))
    return buf.reshape((n,) + shape)


def scatter_step(buf, axis, n, bit):
    me = lax.axis_index(axis)
    half = buf.shape[0] // 2
    mine = (me >> bit) & 1
    keep = lax.dynamic_slice_in_dim(buf, mine * half, half, 0)
    send = lax.dynamic_slice_in_dim(buf, (1 - mine) * half, half, 0)
    return keep + lax.ppermute(send, axis, xor_pairs(n, bit))


def scatter_sum_ordered(x, axis, bits):
    me = lax.axis_index(axis)
    n = x.shape[0]
    buf = x
    for bit in bits:
        half = buf.shape[0] // 2
        mine = (me >> bit) & 1
        keep = lax.dynamic_slice_in_dim(buf, mine * half, half, 0)
        send = lax.dynamic_slice_in_dim(buf, (1 - mine) * half, half, 0)
        buf = keep + lax.ppermute(send, axis, xor_pairs(n, bit))
    return buf[0]


def position(d, bits):
    k = len(bits)
    return sum(((d >> bit) & 1) << (k - 1 - t) for t, bit in enumerate(bits))


def index_bits(n):
    return list(range(n.bit_length() - 1))


def project_kernel(p_ref, w_ref, l_ref, gm_ref, *pt_refs, n_seq, orders):
    rows = p_ref.shape[0]
    width = p_ref.shape[1]
    per_block = width // 16
    half = C // len(orders)
    for i in range(rows):
        prod = lax.dot_general(
            w_ref[...], p_ref[i], (((1,), (1,)), ((), ())), preferred_element_type=jnp.float32
        )
        grad = (prod / n_seq).astype(jnp.bfloat16)
        for e in range(C):
            gm_ref[e, i * C:(i + 1) * C, :] = grad[e * C:(e + 1) * C, :]
    first = pl.program_id(0) * per_block
    for e in range(C):
        part = lax.dot_general(
            gm_ref[e], l_ref[...], (((0,), (1,)), ((), ())), preferred_element_type=jnp.float32
        )
        part = part.reshape(per_block, 16, part.shape[1])
        h = e // half
        for local in range(per_block):
            pt_refs[h][position(first + local, orders[h]), e % half] = part[local]


def left_kernel(gm_ref, rt_ref, out_ref):
    @pl.when(pl.program_id(0) == 0)
    def _():
        out_ref[...] = jnp.zeros_like(out_ref)

    width = gm_ref.shape[2]
    acc = out_ref[...]
    for e in range(gm_ref.shape[0]):
        right_e = rt_ref[:, e, :, :].reshape(width, rt_ref.shape[3])
        acc = acc + jnp.dot(gm_ref[e], right_e, preferred_element_type=jnp.float32)
    out_ref[...] = acc


def per_device(left_proj, right_proj, pair_cot, out_weight):
    n_seq = left_proj.shape[0]
    own_rows = pair_cot.shape[0]
    total = pair_cot.shape[1]
    p_size = pair_cot.shape[2]
    n = lax.axis_size("row")
    bits = index_bits(n)
    block = math.gcd(total, 256)
    steps = total // block
    per_dev = right_proj.shape[1] // C

    right_t = right_proj.reshape(n_seq, per_dev, C).transpose(2, 1, 0)
    swapped = bits[:1] + bits[1:3][::-1] + bits[3:]
    orders = (tuple(bits), tuple(swapped))
    half = C // len(orders)
    early = 2
    weight_ec = out_weight.reshape(C, C, p_size).transpose(1, 0, 2).reshape(C * C, p_size)
    right_t, weight_ec = lax.optimization_barrier((right_t, weight_ec))
    gathers = [(right_t[h * half:(h + 1) * half][None], []) for h in range(len(orders))]
    for h in range(len(orders)):
        for bit in orders[h][::-1][:early]:
            gathers[h] = gather_step(gathers[h], "row", n, bit)

    grad_m, *part_t = pl.pallas_call(
        functools.partial(project_kernel, n_seq=n_seq, orders=orders),
        grid=(steps,),
        in_specs=[
            pl.BlockSpec((own_rows, block, p_size), lambda b: (0, b, 0)),
            pl.BlockSpec((C * C, p_size), lambda b: (0, 0)),
            pl.BlockSpec((n_seq, own_rows * C), lambda b: (0, 0)),
        ],
        out_specs=[
            pl.BlockSpec((C, own_rows * C, block), lambda b: (0, 0, b)),
        ]
        + [pl.BlockSpec((total // 16, half, 16, n_seq), lambda b: (0, 0, 0, 0))] * len(orders),
        out_shape=[
            jax.ShapeDtypeStruct((C, own_rows * C, total), jnp.bfloat16),
        ]
        + [jax.ShapeDtypeStruct((total // 16, half, 16, n_seq), jnp.float32)] * len(orders),
        compiler_params=pltpu.CompilerParams(vmem_limit_bytes=56 * 1024 * 1024),
        cost_estimate=pl.CostEstimate(
            flops=2 * own_rows * total * C * C * (p_size + n_seq),
            transcendentals=0,
            bytes_accessed=2 * own_rows * total * (p_size + C * C) + 4 * total * C * n_seq,
        ),
    )(pair_cot, weight_ec, left_proj)

    scatters = [scatter_step(part_t[h], "row", n, orders[h][0]) for h in range(len(orders))]
    bufs = [g[0] for g in gathers]
    scatters, bufs = lax.optimization_barrier((scatters, bufs))
    gathers = [(bufs[h], gathers[h][1]) for h in range(len(orders))]
    for h in range(len(orders)):
        for bit in orders[h][::-1][early:]:
            gathers[h] = gather_step(gathers[h], "row", n, bit)
    right_blocks = jnp.concatenate(
        [gather_finish(gathers[h], n, right_t[:half].shape) for h in range(len(orders))], 1
    )
    for h in range(len(orders)):
        for bit in orders[h][1:]:
            scatters[h] = scatter_step(scatters[h], "row", n, bit)
    summed = jnp.concatenate([scatters[h][0] for h in range(len(orders))], 0)
    grad_right = summed.transpose(2, 1, 0).reshape(n_seq, per_dev * C).astype(jnp.bfloat16)

    left_t = pl.pallas_call(
        left_kernel,
        grid=(steps,),
        in_specs=[
            pl.BlockSpec((C, own_rows * C, block), lambda b: (0, 0, b)),
            pl.BlockSpec((block // 16, C, 16, n_seq), lambda b: (b, 0, 0, 0)),
        ],
        out_specs=pl.BlockSpec((own_rows * C, n_seq), lambda b: (0, 0)),
        out_shape=jax.ShapeDtypeStruct((own_rows * C, n_seq), jnp.float32),
        compiler_params=pltpu.CompilerParams(vmem_limit_bytes=56 * 1024 * 1024),
        cost_estimate=pl.CostEstimate(
            flops=2 * own_rows * total * C * C * n_seq,
            transcendentals=0,
            bytes_accessed=2 * own_rows * total * C * C + 2 * total * C * n_seq,
        ),
    )(grad_m, right_blocks)
    grad_left = left_t.T.astype(jnp.bfloat16)
    return (grad_left, grad_right)


def solution(mesh):
    return jax.shard_map(
        per_device,
        mesh=mesh,
        in_specs=(P("groups", "row"), P("groups", "row"), P(("groups", "row"), None, None), P()),
        out_specs=(P("groups", "row"), P("groups", "row")),
        check_vma=False,
    )
```

```python
import functools
import math

import jax
import jax.numpy as jnp
from jax import lax
from jax.experimental import pallas as pl
from jax.experimental.pallas import tpu as pltpu
from jax.sharding import PartitionSpec as P

C = 32


def xor_pairs(n, bit):
    return [(i, i ^ (1 << bit)) for i in range(n)]


def gather_blocks(x, axis, n, bits):
    me = lax.axis_index(axis)
    buf = x[None]
    done = []
    for bit in bits:
        other = lax.ppermute(buf, axis, xor_pairs(n, bit))
        mine = (me >> bit) & 1
        low = jnp.where(mine == 0, buf, other)
        high = jnp.where(mine == 0, other, buf)
        buf = jnp.concatenate([low, high], 0)
        done = [bit] + done
    k = len(done)
    buf = buf.reshape((2,) * k + x.shape)
    order = sorted(range(k), key=lambda t: -done[t])
    buf = buf.transpose(order + list(range(k, k + x.ndim)))
    return buf.reshape((n,) + x.shape)


def scatter_sum(x, axis, n, bits):
    me = lax.axis_index(axis)
    k = n.bit_length() - 1
    buf = x.reshape((2,) * k + x.shape[1:])
    left = list(range(k - 1, -1, -1))
    for bit in bits:
        t = left.index(bit)
        mine = (me >> bit) & 1
        moved = jnp.moveaxis(buf, t, 0)
        keep = lax.dynamic_index_in_dim(moved, mine, 0, keepdims=False)
        send = lax.dynamic_index_in_dim(moved, 1 - mine, 0, keepdims=False)
        buf = keep + lax.ppermute(send, axis, xor_pairs(n, bit))
        left.pop(t)
    return buf


def gather_step(state, axis, n, bit):
    buf, done = state
    me = lax.axis_index(axis)
    other = lax.ppermute(buf, axis, xor_pairs(n, bit))
    mine = (me >> bit) & 1
    low = jnp.where(mine == 0, buf, other)
    high = jnp.where(mine == 0, other, buf)
    return jnp.concatenate([low, high], 0), [bit] + done


def gather_finish(state, n, shape):
    buf, done = state
    k = len(done)
    buf = buf.reshape((2,) * k + shape)
    order = sorted(range(k), key=lambda t: -done[t])
    buf = buf.transpose(order + list(range(k, k + len(shape))))
    return buf.reshape((n,) + shape)


def scatter_step(buf, axis, n, bit):
    me = lax.axis_index(axis)
    half = buf.shape[0] // 2
    mine = (me >> bit) & 1
    keep = lax.dynamic_slice_in_dim(buf, mine * half, half, 0)
    send = lax.dynamic_slice_in_dim(buf, (1 - mine) * half, half, 0)
    return keep + lax.ppermute(send, axis, xor_pairs(n, bit))


def scatter_sum_ordered(x, axis, bits):
    me = lax.axis_index(axis)
    n = x.shape[0]
    buf = x
    for bit in bits:
        half = buf.shape[0] // 2
        mine = (me >> bit) & 1
        keep = lax.dynamic_slice_in_dim(buf, mine * half, half, 0)
        send = lax.dynamic_slice_in_dim(buf, (1 - mine) * half, half, 0)
        buf = keep + lax.ppermute(send, axis, xor_pairs(n, bit))
    return buf[0]


def position(d, bits):
    k = len(bits)
    return sum(((d >> bit) & 1) << (k - 1 - t) for t, bit in enumerate(bits))


def index_bits(n):
    return list(range(n.bit_length() - 1))


def project_kernel(p_ref, w_ref, l_ref, gm_ref, *pt_refs, n_seq, orders):
    rows = p_ref.shape[0]
    width = p_ref.shape[1]
    per_block = width // 16
    half = C // len(orders)
    for i in range(rows):
        prod = lax.dot_general(
            w_ref[...], p_ref[i], (((1,), (1,)), ((), ())), preferred_element_type=jnp.float32
        )
        grad = (prod / n_seq).astype(jnp.bfloat16)
        for e in range(C):
            gm_ref[e, i * C:(i + 1) * C, :] = grad[e * C:(e + 1) * C, :]
    first = pl.program_id(0) * per_block
    for e in range(C):
        part = lax.dot_general(
            gm_ref[e], l_ref[...], (((0,), (1,)), ((), ())), preferred_element_type=jnp.float32
        )
        part = part.reshape(per_block, 16, part.shape[1])
        h = e // half
        for local in range(per_block):
            pt_refs[h][position(first + local, orders[h]), e % half] = part[local]


def left_kernel(gm_ref, rt_ref, out_ref):
    @pl.when(pl.program_id(0) == 0)
    def _():
        out_ref[...] = jnp.zeros_like(out_ref)

    width = gm_ref.shape[2]
    acc = out_ref[...]
    for e in range(gm_ref.shape[0]):
        right_e = rt_ref[:, e, :, :].reshape(width, rt_ref.shape[3])
        acc = acc + jnp.dot(gm_ref[e], right_e, preferred_element_type=jnp.float32)
    out_ref[...] = acc


def per_device(left_proj, right_proj, pair_cot, out_weight):
    n_seq = left_proj.shape[0]
    own_rows = pair_cot.shape[0]
    total = pair_cot.shape[1]
    p_size = pair_cot.shape[2]
    n = lax.axis_size("row")
    bits = index_bits(n)
    block = math.gcd(total, 256)
    steps = total // block
    per_dev = right_proj.shape[1] // C

    right_t = right_proj.reshape(n_seq, per_dev, C).transpose(2, 1, 0)
    swapped = bits[:1] + bits[2:] + bits[1:2]
    orders = (tuple(bits), tuple(swapped))
    half = C // len(orders)
    early = 2
    gathers = [(right_t[h * half:(h + 1) * half][None], []) for h in range(len(orders))]
    for h in range(len(orders)):
        for bit in orders[h][::-1][:early]:
            gathers[h] = gather_step(gathers[h], "row", n, bit)

    weight_ec = out_weight.reshape(C, C, p_size).transpose(1, 0, 2).reshape(C * C, p_size)

    grad_m, *part_t = pl.pallas_call(
        functools.partial(project_kernel, n_seq=n_seq, orders=orders),
        grid=(steps,),
        in_specs=[
            pl.BlockSpec((own_rows, block, p_size), lambda b: (0, b, 0)),
            pl.BlockSpec((C * C, p_size), lambda b: (0, 0)),
            pl.BlockSpec((n_seq, own_rows * C), lambda b: (0, 0)),
        ],
        out_specs=[
            pl.BlockSpec((C, own_rows * C, block), lambda b: (0, 0, b)),
        ]
        + [pl.BlockSpec((total // 16, half, 16, n_seq), lambda b: (0, 0, 0, 0))] * len(orders),
        out_shape=[
            jax.ShapeDtypeStruct((C, own_rows * C, total), jnp.bfloat16),
        ]
        + [jax.ShapeDtypeStruct((total // 16, half, 16, n_seq), jnp.float32)] * len(orders),
        compiler_params=pltpu.CompilerParams(vmem_limit_bytes=56 * 1024 * 1024),
        cost_estimate=pl.CostEstimate(
            flops=2 * own_rows * total * C * C * (p_size + n_seq),
            transcendentals=0,
            bytes_accessed=2 * own_rows * total * (p_size + C * C) + 4 * total * C * n_seq,
        ),
    )(pair_cot, weight_ec, left_proj)

    scatters = [scatter_step(part_t[h], "row", n, orders[h][0]) for h in range(len(orders))]
    bufs = [g[0] for g in gathers]
    scatters, bufs = lax.optimization_barrier((scatters, bufs))
    gathers = [(bufs[h], gathers[h][1]) for h in range(len(orders))]
    for h in range(len(orders)):
        for bit in orders[h][::-1][early:]:
            gathers[h] = gather_step(gathers[h], "row", n, bit)
    right_blocks = jnp.concatenate(
        [gather_finish(gathers[h], n, right_t[:half].shape) for h in range(len(orders))], 1
    )
    for h in range(len(orders)):
        for bit in orders[h][1:]:
            scatters[h] = scatter_step(scatters[h], "row", n, bit)
    summed = jnp.concatenate([scatters[h][0] for h in range(len(orders))], 0)
    grad_right = summed.transpose(2, 1, 0).reshape(n_seq, per_dev * C).astype(jnp.bfloat16)

    left_t = pl.pallas_call(
        left_kernel,
        grid=(steps,),
        in_specs=[
            pl.BlockSpec((C, own_rows * C, block), lambda b: (0, 0, b)),
            pl.BlockSpec((block // 16, C, 16, n_seq), lambda b: (b, 0, 0, 0)),
        ],
        out_specs=pl.BlockSpec((own_rows * C, n_seq), lambda b: (0, 0)),
        out_shape=jax.ShapeDtypeStruct((own_rows * C, n_seq), jnp.float32),
        compiler_params=pltpu.CompilerParams(vmem_limit_bytes=56 * 1024 * 1024),
        cost_estimate=pl.CostEstimate(
            flops=2 * own_rows * total * C * C * n_seq,
            transcendentals=0,
            bytes_accessed=2 * own_rows * total * C * C + 2 * total * C * n_seq,
        ),
    )(grad_m, right_blocks)
    grad_left = left_t.T.astype(jnp.bfloat16)
    return (grad_left, grad_right)


def solution(mesh):
    return jax.shard_map(
        per_device,
        mesh=mesh,
        in_specs=(P("groups", "row"), P("groups", "row"), P(("groups", "row"), None, None), P()),
        out_specs=(P("groups", "row"), P("groups", "row")),
        check_vma=False,
    )
```
